32 devices in a mesh: row: 8 (over z, y), col: 4 (over x, core).
Axes of the slice: x: 2, y: 2, z: 4, core: 2. Of those that a mesh axis runs over, the one named last changes fastest.
Arguments:
- features: bfloat16 [4, 8192, 128], P('col', 'row'), may hold values from -6 to 6
- w_self: bfloat16 [128, 256], replicated, may hold values from -0.5 to 0.5
- w_neigh: bfloat16 [128, 256], replicated, may hold values from -2 to 2
- bias: float32 [256], replicated, may hold values from -3 to 3
- blocks: bfloat16 [8, 4, 320, 128, 128], P('row', 'col')
- blk_row: int32 [8, 4, 320], P('row', 'col'), may hold values from 0 to 31
- blk_slot: int32 [8, 4, 320], P('row', 'col'), may hold values from 0 to 15, as said below
- counts: int32 [8, 4, 1], P('row', 'col'), may hold values from 16 to 320, as said below
- col_list: int32 [8, 4, 8, 2], P('row', 'col'), may hold values from 0 to 7, as said below
- cotangent: bfloat16 [4, 8192, 256], P('col', 'row'), may hold values from -6 to 6
Outputs:
- output: bfloat16 [4, 8192, 256], P('col', 'row')
- grad_feats: bfloat16 [4, 8192, 128], P('col', 'row')
- grad_self: float32 [128, 256], replicated
- grad_neigh: float32 [128, 256], replicated
- grad_bias: float32 [256], replicated
The draws below stay inside these ranges and needn't reach their ends.
Inputs may be any that keep to these rules, and one draw needn't show every extreme that they name: `col_list`: for each tile and owner the 2 entries are distinct. `blk_slot`: the first 16 slots of each tile name every read block once, in some order. `counts`: some tile has all 320 slots live.
All inputs are finite; a program needn't handle non-finite values.
Results may differ from the reference program's by a relative error of at most 0.0059.
Values may be sent and summed in bfloat16 or wider, within the bound.
No kernel may reach another device: no remote copies, remote signals or barrier semaphores. Data moves between devices by JAX's collectives and lax.ppermute only.
A program may use at most 128 MiB of HBM per device.

```python
import math
import jax
import jax.numpy as jnp
from jax import lax

D_IN = 128
HID = 256
BLK = 128
NODE_DEV = 1024
PICKS = 2
KB = 320
NODES = 32768
OWN_BLOCKS = 8
ROW_BLOCKS = 32
FETCH = 16
N_ROW = 8
N_COL = 4


def draw_blocks(key, part):
    key = jax.random.fold_in(key, 21)
    first_key, second_key = jax.random.split(key, 2)
    shape = (N_ROW, N_COL, KB, BLK, BLK)
    weights = jax.random.uniform(first_key, shape, jnp.float32)
    keep_share = min(0.5, 2.0 / BLK)
    kept_mask = (jax.random.uniform(second_key, shape, jnp.float32) < keep_share).astype(jnp.float32)
    ramp = 1.0 + 2.0 * jnp.arange(N_COL, dtype=jnp.float32) / max(N_COL - 1, 1)
    weights = weights * kept_mask * ramp[None, :, None, None, None]
    return weights.astype(jnp.bfloat16)


def draw_blk_row(key, part):
    key = jax.random.fold_in(key, 22)
    values = jax.random.randint(key, (N_ROW, N_COL, KB), 0, ROW_BLOCKS, jnp.int32)
    values = values.at[0, 0, 0].set(ROW_BLOCKS - 1)
    return values.at[0, 0, 1].set(0)


def draw_blk_slot(key, part):
    key = jax.random.fold_in(key, 23)
    first_key, second_key = jax.random.split(key)
    tile_keys = jax.random.split(first_key, N_ROW * N_COL)
    leading = jax.vmap(lambda single: jax.random.permutation(single, FETCH))(tile_keys).astype(jnp.int32)
    leading = leading.reshape(N_ROW, N_COL, FETCH)
    rest = jax.random.randint(second_key, (N_ROW, N_COL, KB - FETCH), 0, FETCH, jnp.int32)
    return jnp.concatenate([leading, rest], axis=2)


def draw_counts(key, part):
    key = jax.random.fold_in(key, 24)
    values = jax.random.randint(key, (N_ROW, N_COL, 1), FETCH, KB + 1, jnp.int32)
    return values.at[0, 0, 0].set(KB)


def draw_col_list(key, part):
    key = jax.random.fold_in(key, 25)
    all_keys = jax.random.split(key, N_ROW * N_COL * N_ROW)
    chosen = jax.vmap(lambda single: jax.random.permutation(single, OWN_BLOCKS)[:PICKS])(all_keys).astype(jnp.int32)
    chosen = chosen.reshape(N_ROW, N_COL, N_ROW, PICKS)
    chosen = chosen.at[0, 0, 0].set(jnp.arange(PICKS, dtype=jnp.int32) + OWN_BLOCKS - PICKS)
    return chosen.at[0, 0, 1].set(jnp.arange(PICKS, dtype=jnp.int32))


def block_levels(rng, extent, pieces, low, largest):
    loudness, own = 1.0, jax.random.fold_in(rng, 6)
    for axis_at, shards_of in pieces:
        draws = jnp.exp(jax.random.uniform(jax.random.fold_in(own, axis_at), (shards_of,), jnp.float32, low / len(pieces), largest / len(pieces)))
        loudness = loudness * jnp.repeat(draws, extent[axis_at] // shards_of).reshape([-1 if axis == axis_at else 1 for axis in range(len(extent))])
    return loudness


def bell_draw(key, dims, deviation, reach, shards=(), kind=jnp.bfloat16):
    result = jax.random.normal(key, dims, jnp.float32) * deviation
    if len(shards) > 0:
        result = block_levels(key, dims, shards, -0.22, 0.18) * result
    return jnp.clip(result, min=-reach, max=reach).astype(kind)


def setup_inputs(seed: int = 0) -> dict:
    key_of = jax.random.split(jax.random.key(seed), 11)
    return {
        "features": bell_draw(key_of[0], (N_COL, N_ROW * NODE_DEV, D_IN), 1.0, 6.0, ((0, 4), (1, 8))),
        "w_self": bell_draw(key_of[1], (D_IN, HID), D_IN ** -0.5, 0.5),
        "w_neigh": bell_draw(key_of[2], (D_IN, HID), (D_IN // 16) ** -0.5, 2.0),
        "bias": bell_draw(key_of[3], (HID,), 0.5, 3.0, (), jnp.float32),
        "blocks": draw_blocks(jax.random.fold_in(key_of[10], 71), 0),
        "blk_row": draw_blk_row(jax.random.fold_in(key_of[10], 71), 0),
        "blk_slot": draw_blk_slot(jax.random.fold_in(key_of[10], 71), 0),
        "counts": draw_counts(jax.random.fold_in(key_of[10], 71), 0),
        "col_list": draw_col_list(jax.random.fold_in(key_of[10], 71), 0),
        "cotangent": bell_draw(key_of[9], (N_COL, N_ROW * NODE_DEV, HID), 1.0, 6.0, ((0, 4), (1, 8))),
    }


def gelu_tanh(values):
    return jax.nn.gelu(values, approximate=True)

def reference(features, w_self, w_neigh, bias, blocks, blk_row, blk_slot, counts, col_list, cotangent):
    owners = jnp.repeat(jnp.arange(N_ROW, dtype=jnp.int32), PICKS) * OWN_BLOCKS
    slot_ids = jnp.arange(KB, dtype=jnp.int32)

    def tile_view(tile):
        row_index = tile // N_COL
        col_index = tile % N_COL
        live_mask = (slot_ids < counts[row_index, col_index, 0]).astype(jnp.float32)
        adjacency = blocks[row_index, col_index].astype(jnp.float32) * live_mask[:, None, None]
        fetch_ids = owners + col_list[row_index, col_index].reshape(-1).astype(jnp.int32)
        block_ids = fetch_ids[blk_slot[row_index, col_index]]
        return (row_index, col_index, adjacency, block_ids, blk_row[row_index, col_index])

    def forward_tile(tile, carry):
        summed, degree = carry
        row_index, col_index, adjacency, block_ids, row_ids = tile_view(tile)
        column = lax.dynamic_index_in_dim(features, col_index, 0, keepdims=False)
        column = column.reshape(N_ROW * OWN_BLOCKS, BLK, D_IN).astype(jnp.float32)
        gathered = column[block_ids]
        products = jnp.einsum('kij,kjd->kid', adjacency, gathered)
        part_sum = jax.ops.segment_sum(products, row_ids, num_segments=ROW_BLOCKS).reshape(N_COL, NODE_DEV, D_IN)
        part_deg = jax.ops.segment_sum(lax.optimization_barrier(jnp.sum(adjacency, axis=2)), row_ids, num_segments=ROW_BLOCKS).reshape(N_COL, NODE_DEV)
        return (summed.at[:, row_index].add(part_sum), degree.at[:, row_index].add(part_deg))
    start_sum = jnp.zeros((N_COL, N_ROW, NODE_DEV, D_IN), jnp.float32)
    start_deg = jnp.zeros((N_COL, N_ROW, NODE_DEV), jnp.float32)
    summed, degree = lax.fori_loop(0, N_ROW * N_COL, forward_tile, (start_sum, start_deg))
    divisor = 1.0 + degree.reshape(-1)
    flat_feats = features.reshape(-1, D_IN)
    neighbors = (summed.reshape(-1, D_IN) / divisor[:, None]).astype(jnp.bfloat16)
    hidden = jnp.dot(flat_feats, w_self, preferred_element_type=jnp.float32) + jnp.dot(neighbors, w_neigh, preferred_element_type=jnp.float32) + bias
    output, pullback = jax.vjp(gelu_tanh, hidden)
    grad_hidden = pullback(cotangent.reshape(-1, HID).astype(jnp.float32))[0]
    grad_round = grad_hidden.astype(jnp.bfloat16)
    factor = 1.0 / math.sqrt(NODES)
    grad_self = jnp.dot(flat_feats.T, grad_round, preferred_element_type=jnp.float32) * factor
    grad_neigh = jnp.dot(neighbors.T, grad_round, preferred_element_type=jnp.float32) * factor
    grad_bias = lax.optimization_barrier(jnp.sum(grad_round.astype(jnp.float32), axis=0)) * factor
    grad_agg = (jnp.dot(grad_round, w_neigh.T, preferred_element_type=jnp.float32) / divisor[:, None]).astype(jnp.bfloat16)
    grad_agg = grad_agg.reshape(N_COL, N_ROW, NODE_DEV, D_IN)

    def backward_tile(tile, adjoint):
        row_index, col_index, adjacency, block_ids, row_ids = tile_view(tile)
        panel = grad_agg[:, row_index].reshape(ROW_BLOCKS, BLK, D_IN).astype(jnp.float32)
        row_pieces = panel[row_ids]
        backward = jnp.einsum('kij,kid->kjd', adjacency, row_pieces)
        spread = jax.ops.segment_sum(backward, block_ids, num_segments=N_ROW * OWN_BLOCKS)
        return adjoint.at[col_index].add(spread)
    start_adj = jnp.zeros((N_COL, N_ROW * OWN_BLOCKS, BLK, D_IN), jnp.float32)
    adjoint = lax.fori_loop(0, N_ROW * N_COL, backward_tile, start_adj)
    grad_feats = jnp.dot(grad_round, w_self.T, preferred_element_type=jnp.float32) + adjoint.reshape(-1, D_IN)
    return (output.astype(jnp.bfloat16).reshape(N_COL, N_ROW * NODE_DEV, HID), grad_feats.astype(jnp.bfloat16).reshape(N_COL, N_ROW * NODE_DEV, D_IN), grad_self, grad_neigh, grad_bias)
```

```python
import functools
import math

import jax
import jax.numpy as jnp
from jax import lax
from jax.experimental import pallas as pl
from jax.experimental.pallas import tpu as pltpu
from jax.sharding import PartitionSpec as P

GROUP = 32


def gelu_tanh(values):
    return jax.nn.gelu(values, approximate=True)


def select_rows(indices, table, total):
    picker = (indices[:, None] == jnp.arange(total, dtype=jnp.int32)[None, :]).astype(table.dtype)
    flat = table.reshape(total, -1)
    taken = jnp.dot(picker, flat, preferred_element_type=jnp.float32).astype(table.dtype)
    return taken.reshape((indices.shape[0],) + table.shape[1:])


def group_rows(indices, values, total):
    grouper = (jnp.arange(total, dtype=jnp.int32)[:, None] == indices[None, :]).astype(jnp.float32)
    flat = values.reshape(values.shape[0], -1)
    added = jnp.dot(
        grouper, flat, precision=lax.Precision.HIGHEST, preferred_element_type=jnp.float32
    )
    return added.reshape((total,) + values.shape[1:])


def _live_group(g, count_ref):
    return jnp.minimum(g, (count_ref[0] - 1) // GROUP)


def _forward_kernel(count_ref, row_ref, slot_ref, blk_ref, feat_ref, sum_ref, deg_ref):
    g = pl.program_id(0)

    @pl.when(g == 0)
    def _():
        sum_ref[...] = jnp.zeros_like(sum_ref)
        deg_ref[...] = jnp.zeros_like(deg_ref)

    count = count_ref[0]
    ones = jnp.ones((8, blk_ref.shape[-1]), jnp.bfloat16)
    for j in range(GROUP):
        k = g * GROUP + j

        @pl.when(k < count)
        def _():
            blk = blk_ref[j]
            r = row_ref[k]
            s = slot_ref[k]
            sum_ref[r] += jnp.dot(blk, feat_ref[s], preferred_element_type=jnp.float32)
            deg_ref[r] += lax.dot_general(
                ones, blk, (((1,), (1,)), ((), ())), preferred_element_type=jnp.float32
            )


def _backward_kernel(count_ref, row_ref, slot_ref, blk_ref, grad_ref, out_ref):
    g = pl.program_id(0)

    @pl.when(g == 0)
    def _():
        out_ref[...] = jnp.zeros_like(out_ref)

    count = count_ref[0]
    for j in range(GROUP):
        k = g * GROUP + j

        @pl.when(k < count)
        def _():
            blk = blk_ref[j]
            r = row_ref[k]
            s = slot_ref[k]
            out_ref[s] += lax.dot_general(
                blk, grad_ref[r], (((0,), (0,)), ((), ())), preferred_element_type=jnp.float32
            )


def aggregate_forward(counts, rows, slots, blocks, fetched, panel_blocks):
    slot_total, bs, _ = blocks.shape
    fetch_total, _, width = fetched.shape
    grid_spec = pltpu.PrefetchScalarGridSpec(
        num_scalar_prefetch=3,
        grid=(slot_total // GROUP,),
        in_specs=[
            pl.BlockSpec((GROUP, bs, bs), lambda g, c, r, s: (_live_group(g, c), 0, 0)),
            pl.BlockSpec((fetch_total, bs, width), lambda g, c, r, s: (0, 0, 0)),
        ],
        out_specs=[
            pl.BlockSpec((panel_blocks, bs, width), lambda g, c, r, s: (0, 0, 0)),
            pl.BlockSpec((panel_blocks, 8, bs), lambda g, c, r, s: (0, 0, 0)),
        ],
    )
    flops = 2 * slot_total * bs * bs * (width + 8)
    return pl.pallas_call(
        _forward_kernel,
        grid_spec=grid_spec,
        out_shape=[
            jax.ShapeDtypeStruct((panel_blocks, bs, width), jnp.float32),
            jax.ShapeDtypeStruct((panel_blocks, 8, bs), jnp.float32),
        ],
        compiler_params=pltpu.CompilerParams(dimension_semantics=("arbitrary",)),
        cost_estimate=pl.CostEstimate(
            flops=flops,
            bytes_accessed=blocks.size * 2 + fetched.size * 2 + panel_blocks * bs * (width + 8) * 4,
            transcendentals=0,
        ),
    )(counts, rows, slots, blocks, fetched)


def aggregate_backward(counts, rows, slots, blocks, grad_panel, fetch_total):
    slot_total, bs, _ = blocks.shape
    panel_blocks, _, width = grad_panel.shape
    grid_spec = pltpu.PrefetchScalarGridSpec(
        num_scalar_prefetch=3,
        grid=(slot_total // GROUP,),
        in_specs=[
            pl.BlockSpec((GROUP, bs, bs), lambda g, c, r, s: (_live_group(g, c), 0, 0)),
            pl.BlockSpec((panel_blocks, bs, width), lambda g, c, r, s: (0, 0, 0)),
        ],
        out_specs=pl.BlockSpec((fetch_total, bs, width), lambda g, c, r, s: (0, 0, 0)),
    )
    return pl.pallas_call(
        _backward_kernel,
        grid_spec=grid_spec,
        out_shape=jax.ShapeDtypeStruct((fetch_total, bs, width), jnp.float32),
        compiler_params=pltpu.CompilerParams(dimension_semantics=("arbitrary",)),
        cost_estimate=pl.CostEstimate(
            flops=2 * slot_total * bs * bs * width,
            bytes_accessed=blocks.size * 2 + grad_panel.size * 2 + fetch_total * bs * width * 4,
            transcendentals=0,
        ),
    )(counts, rows, slots, blocks, grad_panel)


def all_sum(values, axes):
    for name in axes:
        size = lax.axis_size(name)
        step = 1
        while step < size:
            pairs = [(i, i ^ step) for i in range(size)]
            values = values + lax.ppermute(values, name, pairs)
            step *= 2
    return values


def on_device(
    features, w_self, w_neigh, bias, blocks, blk_row, blk_slot, counts, col_list, cotangent
):
    own_feats = features[0]
    node_count, feat_width = own_feats.shape
    block_size = blocks.shape[-1]
    owned_count = node_count // block_size
    row_count = lax.axis_size("row")
    col_count = lax.axis_size("col")
    picks_each = col_list.shape[-1]
    fetch_total = row_count * picks_each
    panel_blocks = col_count * owned_count
    wanted = col_list[0, 0]
    asked_for = lax.all_to_all(wanted, "row", split_axis=0, concat_axis=0, tiled=True)
    block_rows = blk_row[0, 0]
    block_slots = blk_slot[0, 0]
    live_count = counts[0, 0]
    own_blocks = own_feats.reshape(owned_count, block_size, feat_width)
    outgoing = select_rows(asked_for.reshape(-1), own_blocks, owned_count)
    outgoing = outgoing.reshape(row_count, picks_each, block_size, feat_width)
    arrived = lax.all_to_all(outgoing, "row", split_axis=0, concat_axis=0, tiled=True)
    fetched = arrived.reshape(fetch_total, block_size, feat_width)
    part_sums, part_deg = aggregate_forward(
        live_count, block_rows, block_slots, blocks[0, 0], fetched, panel_blocks
    )
    part_sums = part_sums.reshape(col_count, node_count, feat_width)
    part_deg = part_deg[:, 0, :].reshape(col_count, owned_count, block_size)
    part_deg = jnp.pad(part_deg, ((0, 0), (0, 16 - owned_count), (0, 0)))
    packed = jnp.concatenate([part_sums, part_deg], axis=1)
    packed = packed.reshape(col_count * (node_count + 16), feat_width)
    reduced = lax.psum_scatter(packed, "col", scatter_dimension=0, tiled=True)
    summed = reduced[:node_count]
    degree = reduced[node_count : node_count + owned_count].reshape(node_count)
    divisor = 1.0 + degree
    neighbors = (summed / divisor[:, None]).astype(jnp.bfloat16)
    hidden = (
        jnp.dot(own_feats, w_self, preferred_element_type=jnp.float32)
        + jnp.dot(neighbors, w_neigh, preferred_element_type=jnp.float32)
        + bias
    )
    output, pullback = jax.vjp(gelu_tanh, hidden)
    grad_hidden = pullback(cotangent[0].astype(jnp.float32))[0]
    grad_round = grad_hidden.astype(jnp.bfloat16)
    local_self = jnp.einsum("nd,nh->dh", own_feats, grad_round, preferred_element_type=jnp.float32)
    local_neigh = jnp.einsum("nd,nh->dh", neighbors, grad_round, preferred_element_type=jnp.float32)
    local_bias = jnp.sum(grad_round.astype(jnp.float32), axis=0)
    hid = local_bias.shape[0]
    weight_pack = jnp.concatenate(
        [local_self, local_neigh, jnp.broadcast_to(local_bias[None], (8, hid))], axis=0
    )
    weight_pack = all_sum(weight_pack, ("col", "row"))
    factor = 1.0 / math.sqrt(node_count * row_count * col_count)
    grad_self = weight_pack[:feat_width] * factor
    grad_neigh = weight_pack[feat_width : 2 * feat_width] * factor
    grad_bias = weight_pack[2 * feat_width] * factor
    grad_agg = (
        jnp.einsum("nh,dh->nd", grad_round, w_neigh, preferred_element_type=jnp.float32)
        / divisor[:, None]
    )
    grad_agg = grad_agg.astype(jnp.bfloat16)
    adjoint_panel = lax.all_gather(grad_agg, "col", axis=0, tiled=True)
    per_slot = aggregate_backward(
        live_count,
        block_rows,
        block_slots,
        blocks[0, 0],
        adjoint_panel.reshape(panel_blocks, block_size, feat_width),
        fetch_total,
    )
    per_slot = per_slot.reshape(row_count, picks_each, block_size, feat_width)
    returned = lax.all_to_all(per_slot, "row", split_axis=0, concat_axis=0, tiled=True)
    incoming = group_rows(
        asked_for.reshape(-1),
        returned.reshape(fetch_total, block_size, feat_width),
        owned_count,
    )
    incoming = incoming.reshape(node_count, feat_width)
    grad_feats = (
        jnp.einsum("nh,dh->nd", grad_round, w_self, preferred_element_type=jnp.float32) + incoming
    )
    return (
        output.astype(jnp.bfloat16)[None],
        grad_feats.astype(jnp.bfloat16)[None],
        grad_self,
        grad_neigh,
        grad_bias,
    )


def solution(mesh):
    return jax.shard_map(
        on_device,
        mesh=mesh,
        in_specs=(
            P("col", "row", None),
            P(),
            P(),
            P(),
            P("row", "col", None, None, None),
            P("row", "col", None),
            P("row", "col", None),
            P("row", "col", None),
            P("row", "col", None, None),
            P("col", "row", None),
        ),
        out_specs=(P("col", "row", None), P("col", "row", None), P(), P(), P()),
        check_vma=False,
    )
```

```python
import functools
import math

import jax
import jax.numpy as jnp
from jax import lax
from jax.experimental import pallas as pl
from jax.experimental.pallas import tpu as pltpu
from jax.sharding import PartitionSpec as P

GROUP = 32


def gelu_tanh(values):
    return jax.nn.gelu(values, approximate=True)


def select_rows(indices, table, total):
    picker = (indices[:, None] == jnp.arange(total, dtype=jnp.int32)[None, :]).astype(table.dtype)
    flat = table.reshape(total, -1)
    taken = jnp.dot(picker, flat, preferred_element_type=jnp.float32).astype(table.dtype)
    return taken.reshape((indices.shape[0],) + table.shape[1:])


def group_rows(indices, values, total):
    grouper = (jnp.arange(total, dtype=jnp.int32)[:, None] == indices[None, :]).astype(jnp.float32)
    flat = values.reshape(values.shape[0], -1)
    added = jnp.dot(
        grouper, flat, precision=lax.Precision.HIGHEST, preferred_element_type=jnp.float32
    )
    return added.reshape((total,) + values.shape[1:])


def _live_group(g, count_ref):
    return jnp.minimum(g, (count_ref[0] - 1) // GROUP)


def _forward_kernel(count_ref, row_ref, slot_ref, blk_ref, feat_ref, sum_ref, deg_ref):
    g = pl.program_id(0)

    @pl.when(g == 0)
    def _():
        sum_ref[...] = jnp.zeros_like(sum_ref)
        deg_ref[...] = jnp.zeros_like(deg_ref)

    count = count_ref[0]
    ones = jnp.ones((8, blk_ref.shape[-1]), jnp.bfloat16)

    @pl.when(g * GROUP < count)
    def _():
        for j in range(GROUP):
            k = g * GROUP + j
            live = k < count
            blk = blk_ref[j]
            r = row_ref[k]
            s = slot_ref[k]
            prod = jnp.dot(blk, feat_ref[s], preferred_element_type=jnp.float32)
            rsum = lax.dot_general(
                ones, blk, (((1,), (1,)), ((), ())), preferred_element_type=jnp.float32
            )
            sum_ref[r] += jnp.where(live, prod, 0.0)
            deg_ref[r] += jnp.where(live, rsum, 0.0)


def _backward_kernel(count_ref, row_ref, slot_ref, blk_ref, grad_ref, out_ref):
    g = pl.program_id(0)

    @pl.when(g == 0)
    def _():
        out_ref[...] = jnp.zeros_like(out_ref)

    count = count_ref[0]

    @pl.when(g * GROUP < count)
    def _():
        for j in range(GROUP):
            k = g * GROUP + j
            live = k < count
            blk = blk_ref[j]
            r = row_ref[k]
            s = slot_ref[k]
            prod = jnp.dot(grad_ref[r], blk, preferred_element_type=jnp.float32)
            out_ref[s] += jnp.where(live, prod, 0.0)


def aggregate_forward(counts, rows, slots, blocks, fetched, panel_blocks):
    slot_total, bs, _ = blocks.shape
    fetch_total, _, width = fetched.shape
    grid_spec = pltpu.PrefetchScalarGridSpec(
        num_scalar_prefetch=3,
        grid=(slot_total // GROUP,),
        in_specs=[
            pl.BlockSpec((GROUP, bs, bs), lambda g, c, r, s: (_live_group(g, c), 0, 0)),
            pl.BlockSpec((fetch_total, bs, width), lambda g, c, r, s: (0, 0, 0)),
        ],
        out_specs=[
            pl.BlockSpec((panel_blocks, bs, width), lambda g, c, r, s: (0, 0, 0)),
            pl.BlockSpec((panel_blocks, 8, bs), lambda g, c, r, s: (0, 0, 0)),
        ],
    )
    flops = 2 * slot_total * bs * bs * (width + 8)
    return pl.pallas_call(
        _forward_kernel,
        grid_spec=grid_spec,
        out_shape=[
            jax.ShapeDtypeStruct((panel_blocks, bs, width), jnp.float32),
            jax.ShapeDtypeStruct((panel_blocks, 8, bs), jnp.float32),
        ],
        compiler_params=pltpu.CompilerParams(dimension_semantics=("arbitrary",)),
        cost_estimate=pl.CostEstimate(
            flops=flops,
            bytes_accessed=blocks.size * 2 + fetched.size * 2 + panel_blocks * bs * (width + 8) * 4,
            transcendentals=0,
        ),
    )(counts, rows, slots, blocks, fetched)


def aggregate_backward(counts, rows, slots, blocks, grad_panel, fetch_total):
    slot_total, bs, _ = blocks.shape
    panel_blocks, width, _ = grad_panel.shape
    grid_spec = pltpu.PrefetchScalarGridSpec(
        num_scalar_prefetch=3,
        grid=(slot_total // GROUP,),
        in_specs=[
            pl.BlockSpec((GROUP, bs, bs), lambda g, c, r, s: (_live_group(g, c), 0, 0)),
            pl.BlockSpec((panel_blocks, width, bs), lambda g, c, r, s: (0, 0, 0)),
        ],
        out_specs=pl.BlockSpec((fetch_total, width, bs), lambda g, c, r, s: (0, 0, 0)),
    )
    return pl.pallas_call(
        _backward_kernel,
        grid_spec=grid_spec,
        out_shape=jax.ShapeDtypeStruct((fetch_total, width, bs), jnp.float32),
        compiler_params=pltpu.CompilerParams(dimension_semantics=("arbitrary",)),
        cost_estimate=pl.CostEstimate(
            flops=2 * slot_total * bs * bs * width,
            bytes_accessed=blocks.size * 2 + grad_panel.size * 2 + fetch_total * bs * width * 4,
            transcendentals=0,
        ),
    )(counts, rows, slots, blocks, grad_panel)


def all_sum(values, axes):
    for name in axes:
        size = lax.axis_size(name)
        step = 1
        while step < size:
            pairs = [(i, i ^ step) for i in range(size)]
            values = values + lax.ppermute(values, name, pairs)
            step *= 2
    return values


def on_device(
    features, w_self, w_neigh, bias, blocks, blk_row, blk_slot, counts, col_list, cotangent
):
    own_feats = features[0]
    node_count, feat_width = own_feats.shape
    block_size = blocks.shape[-1]
    owned_count = node_count // block_size
    row_count = lax.axis_size("row")
    col_count = lax.axis_size("col")
    picks_each = col_list.shape[-1]
    fetch_total = row_count * picks_each
    panel_blocks = col_count * owned_count
    wanted = col_list[0, 0]
    asked_for = lax.all_to_all(wanted, "row", split_axis=0, concat_axis=0, tiled=True)
    block_rows = blk_row[0, 0]
    block_slots = blk_slot[0, 0]
    live_count = counts[0, 0]
    own_blocks = own_feats.reshape(owned_count, block_size, feat_width)
    outgoing = select_rows(asked_for.reshape(-1), own_blocks, owned_count)
    outgoing = outgoing.reshape(row_count, picks_each, block_size, feat_width)
    arrived = lax.all_to_all(outgoing, "row", split_axis=0, concat_axis=0, tiled=True)
    fetched = arrived.reshape(fetch_total, block_size, feat_width)
    part_sums, part_deg = aggregate_forward(
        live_count, block_rows, block_slots, blocks[0, 0], fetched, panel_blocks
    )
    part_sums = part_sums.reshape(col_count, node_count, feat_width)
    part_deg = part_deg[:, 0, :].reshape(col_count, owned_count, block_size)
    part_deg = jnp.pad(part_deg, ((0, 0), (0, 16 - owned_count), (0, 0)))
    packed = jnp.concatenate([part_sums, part_deg], axis=1)
    packed = packed.reshape(col_count * (node_count + 16), feat_width)
    reduced = lax.psum_scatter(packed, "col", scatter_dimension=0, tiled=True)
    summed = reduced[:node_count]
    degree = reduced[node_count : node_count + owned_count].reshape(node_count)
    divisor = 1.0 + degree
    neighbors = (summed / divisor[:, None]).astype(jnp.bfloat16)
    hidden = (
        jnp.dot(own_feats, w_self, preferred_element_type=jnp.float32)
        + jnp.dot(neighbors, w_neigh, preferred_element_type=jnp.float32)
        + bias
    )
    output, pullback = jax.vjp(gelu_tanh, hidden)
    grad_hidden = pullback(cotangent[0].astype(jnp.float32))[0]
    grad_round = grad_hidden.astype(jnp.bfloat16)
    local_self = jnp.einsum("nd,nh->dh", own_feats, grad_round, preferred_element_type=jnp.float32)
    local_neigh = jnp.einsum("nd,nh->dh", neighbors, grad_round, preferred_element_type=jnp.float32)
    local_bias = jnp.sum(grad_round.astype(jnp.float32), axis=0)
    hid = local_bias.shape[0]
    weight_pack = jnp.concatenate(
        [local_self, local_neigh, jnp.broadcast_to(local_bias[None], (8, hid))], axis=0
    )
    weight_pack = all_sum(weight_pack, ("col", "row"))
    factor = 1.0 / math.sqrt(node_count * row_count * col_count)
    grad_self = weight_pack[:feat_width] * factor
    grad_neigh = weight_pack[feat_width : 2 * feat_width] * factor
    grad_bias = weight_pack[2 * feat_width] * factor
    grad_agg = (
        jnp.einsum("nh,dh->nd", grad_round, w_neigh, preferred_element_type=jnp.float32)
        / divisor[:, None]
    )
    grad_agg = grad_agg.astype(jnp.bfloat16)
    adjoint_panel = lax.all_gather(grad_agg, "col", axis=0, tiled=True)
    panel_t = adjoint_panel.reshape(panel_blocks, block_size, feat_width).transpose(0, 2, 1)
    per_slot_t = aggregate_backward(
        live_count, block_rows, block_slots, blocks[0, 0], panel_t, fetch_total
    )
    per_slot = per_slot_t.transpose(0, 2, 1).reshape(row_count, picks_each, block_size, feat_width)
    returned = lax.all_to_all(per_slot, "row", split_axis=0, concat_axis=0, tiled=True)
    incoming = group_rows(
        asked_for.reshape(-1),
        returned.reshape(fetch_total, block_size, feat_width),
        owned_count,
    )
    incoming = incoming.reshape(node_count, feat_width)
    grad_feats = (
        jnp.einsum("nh,dh->nd", grad_round, w_self, preferred_element_type=jnp.float32) + incoming
    )
    return (
        output.astype(jnp.bfloat16)[None],
        grad_feats.astype(jnp.bfloat16)[None],
        grad_self,
        grad_neigh,
        grad_bias,
    )


def solution(mesh):
    return jax.shard_map(
        on_device,
        mesh=mesh,
        in_specs=(
            P("col", "row", None),
            P(),
            P(),
            P(),
            P("row", "col", None, None, None),
            P("row", "col", None),
            P("row", "col", None),
            P("row", "col", None),
            P("row", "col", None, None),
            P("col", "row", None),
        ),
        out_specs=(P("col", "row", None), P("col", "row", None), P(), P(), P()),
        check_vma=False,
    )
```

```python
import functools
import math

import jax
import jax.numpy as jnp
from jax import lax
from jax.experimental import pallas as pl
from jax.experimental.pallas import tpu as pltpu
from jax.sharding import PartitionSpec as P

GROUP = 32


def gelu_tanh(values):
    return jax.nn.gelu(values, approximate=True)


def select_rows(indices, table, total):
    picker = (indices[:, None] == jnp.arange(total, dtype=jnp.int32)[None, :]).astype(table.dtype)
    flat = table.reshape(total, -1)
    taken = jnp.dot(picker, flat, preferred_element_type=jnp.float32).astype(table.dtype)
    return taken.reshape((indices.shape[0],) + table.shape[1:])


def group_rows(indices, values, total):
    grouper = (jnp.arange(total, dtype=jnp.int32)[:, None] == indices[None, :]).astype(jnp.float32)
    flat = values.reshape(values.shape[0], -1)
    added = jnp.dot(
        grouper, flat, precision=lax.Precision.HIGHEST, preferred_element_type=jnp.float32
    )
    return added.reshape((total,) + values.shape[1:])


def _live_group(g, count_ref):
    return jnp.minimum(g, (count_ref[0] - 1) // GROUP)


def _forward_kernel(count_ref, row_ref, slot_ref, blk_ref, feat_ref, sum_ref, deg_ref):
    g = pl.program_id(0)

    @pl.when(g == 0)
    def _():
        sum_ref[...] = jnp.zeros_like(sum_ref)
        deg_ref[...] = jnp.zeros_like(deg_ref)

    count = count_ref[0]
    ones = jnp.ones((8, blk_ref.shape[-1]), jnp.bfloat16)

    @pl.when(g * GROUP < count)
    def _():
        for j in range(GROUP):
            k = g * GROUP + j
            live = k < count
            blk = blk_ref[j]
            r = row_ref[k]
            s = slot_ref[k]
            prod = jnp.dot(blk, feat_ref[s], preferred_element_type=jnp.float32)
            rsum = lax.dot_general(
                ones, blk, (((1,), (1,)), ((), ())), preferred_element_type=jnp.float32
            )
            sum_ref[r] += jnp.where(live, prod, 0.0)
            deg_ref[r] += jnp.where(live, rsum, 0.0)


def _backward_kernel(count_ref, row_ref, slot_ref, blk_ref, grad_ref, out_ref):
    g = pl.program_id(0)

    @pl.when(g == 0)
    def _():
        out_ref[...] = jnp.zeros_like(out_ref)

    count = count_ref[0]

    @pl.when(g * GROUP < count)
    def _():
        for j in range(GROUP):
            k = g * GROUP + j
            live = k < count
            blk = blk_ref[j]
            r = row_ref[k]
            s = slot_ref[k]
            prod = jnp.dot(grad_ref[r], blk, preferred_element_type=jnp.float32)
            out_ref[s] += jnp.where(live, prod, 0.0)


def aggregate_forward(counts, rows, slots, blocks, fetched, panel_blocks):
    slot_total, bs, _ = blocks.shape
    fetch_total, _, width = fetched.shape
    grid_spec = pltpu.PrefetchScalarGridSpec(
        num_scalar_prefetch=3,
        grid=(slot_total // GROUP,),
        in_specs=[
            pl.BlockSpec((GROUP, bs, bs), lambda g, c, r, s: (_live_group(g, c), 0, 0)),
            pl.BlockSpec((fetch_total, bs, width), lambda g, c, r, s: (0, 0, 0)),
        ],
        out_specs=[
            pl.BlockSpec((panel_blocks, bs, width), lambda g, c, r, s: (0, 0, 0)),
            pl.BlockSpec((panel_blocks, 8, bs), lambda g, c, r, s: (0, 0, 0)),
        ],
    )
    flops = 2 * slot_total * bs * bs * (width + 8)
    return pl.pallas_call(
        _forward_kernel,
        grid_spec=grid_spec,
        out_shape=[
            jax.ShapeDtypeStruct((panel_blocks, bs, width), jnp.float32),
            jax.ShapeDtypeStruct((panel_blocks, 8, bs), jnp.float32),
        ],
        compiler_params=pltpu.CompilerParams(dimension_semantics=("arbitrary",)),
        cost_estimate=pl.CostEstimate(
            flops=flops,
            bytes_accessed=blocks.size * 2 + fetched.size * 2 + panel_blocks * bs * (width + 8) * 4,
            transcendentals=0,
        ),
    )(counts, rows, slots, blocks, fetched)


def aggregate_backward(counts, rows, slots, blocks, grad_panel, fetch_total):
    slot_total, bs, _ = blocks.shape
    panel_blocks, width, _ = grad_panel.shape
    grid_spec = pltpu.PrefetchScalarGridSpec(
        num_scalar_prefetch=3,
        grid=(slot_total // GROUP,),
        in_specs=[
            pl.BlockSpec((GROUP, bs, bs), lambda g, c, r, s: (_live_group(g, c), 0, 0)),
            pl.BlockSpec((panel_blocks, width, bs), lambda g, c, r, s: (0, 0, 0)),
        ],
        out_specs=pl.BlockSpec((fetch_total, width, bs), lambda g, c, r, s: (0, 0, 0)),
    )
    return pl.pallas_call(
        _backward_kernel,
        grid_spec=grid_spec,
        out_shape=jax.ShapeDtypeStruct((fetch_total, width, bs), jnp.float32),
        compiler_params=pltpu.CompilerParams(dimension_semantics=("arbitrary",)),
        cost_estimate=pl.CostEstimate(
            flops=2 * slot_total * bs * bs * width,
            bytes_accessed=blocks.size * 2 + grad_panel.size * 2 + fetch_total * bs * width * 4,
            transcendentals=0,
        ),
    )(counts, rows, slots, blocks, grad_panel)


def exchange_steps(axes):
    steps = []
    for name in axes:
        size = lax.axis_size(name)
        step = 1
        while step < size:
            steps.append((name, size, step))
            step *= 2
    return steps[::-1]


def exchange_add(values, step):
    name, size, offset = step
    pairs = [(i, i ^ offset) for i in range(size)]
    return values + lax.ppermute(values, name, pairs)


def on_device(
    features, w_self, w_neigh, bias, blocks, blk_row, blk_slot, counts, col_list, cotangent
):
    own_feats = features[0]
    node_count, feat_width = own_feats.shape
    block_size = blocks.shape[-1]
    owned_count = node_count // block_size
    row_count = lax.axis_size("row")
    col_count = lax.axis_size("col")
    picks_each = col_list.shape[-1]
    fetch_total = row_count * picks_each
    panel_blocks = col_count * owned_count
    wanted = col_list[0, 0]
    asked_for = lax.all_to_all(wanted, "row", split_axis=0, concat_axis=0, tiled=True)
    block_rows = blk_row[0, 0]
    block_slots = blk_slot[0, 0]
    live_count = counts[0, 0]
    own_blocks = own_feats.reshape(owned_count, block_size, feat_width)
    outgoing = select_rows(asked_for.reshape(-1), own_blocks, owned_count)
    outgoing = outgoing.reshape(row_count, picks_each, block_size, feat_width)
    arrived = lax.all_to_all(outgoing, "row", split_axis=0, concat_axis=0, tiled=True)
    fetched = arrived.reshape(fetch_total, block_size, feat_width)
    part_sums, part_deg = aggregate_forward(
        live_count, block_rows, block_slots, blocks[0, 0], fetched, panel_blocks
    )
    part_sums = part_sums.reshape(col_count, node_count, feat_width)
    part_deg = part_deg[:, 0, :].reshape(col_count, owned_count, block_size)
    part_deg = jnp.pad(part_deg, ((0, 0), (0, 16 - owned_count), (0, 0)))
    packed = jnp.concatenate([part_sums, part_deg], axis=1)
    packed = packed.reshape(col_count * (node_count + 16), feat_width)
    reduced = lax.psum_scatter(packed, "col", scatter_dimension=0, tiled=True)
    summed = reduced[:node_count]
    degree = reduced[node_count : node_count + owned_count].reshape(node_count)
    divisor = 1.0 + degree
    neighbors = (summed / divisor[:, None]).astype(jnp.bfloat16)
    hidden = (
        jnp.dot(own_feats, w_self, preferred_element_type=jnp.float32)
        + jnp.dot(neighbors, w_neigh, preferred_element_type=jnp.float32)
        + bias
    )
    output, pullback = jax.vjp(gelu_tanh, hidden)
    grad_hidden = pullback(cotangent[0].astype(jnp.float32))[0]
    grad_round = grad_hidden.astype(jnp.bfloat16)
    local_self = jnp.einsum("nd,nh->dh", own_feats, grad_round, preferred_element_type=jnp.float32)
    local_neigh = jnp.einsum("nd,nh->dh", neighbors, grad_round, preferred_element_type=jnp.float32)
    local_bias = jnp.sum(grad_round.astype(jnp.float32), axis=0)
    hid = local_bias.shape[0]
    weight_pack = jnp.concatenate(
        [local_self, local_neigh, jnp.broadcast_to(local_bias[None], (8, hid))], axis=0
    )
    steps = exchange_steps(("col", "row"))
    grad_agg = (
        jnp.einsum("nh,dh->nd", grad_round, w_neigh, preferred_element_type=jnp.float32)
        / divisor[:, None]
    )
    grad_agg = grad_agg.astype(jnp.bfloat16)
    adjoint_panel = lax.all_gather(grad_agg, "col", axis=0, tiled=True)
    weight_pack = exchange_add(weight_pack, steps[0])
    weight_pack, adjoint_panel = lax.optimization_barrier((weight_pack, adjoint_panel))
    panel_t = adjoint_panel.reshape(panel_blocks, block_size, feat_width).transpose(0, 2, 1)
    per_slot_t = aggregate_backward(
        live_count, block_rows, block_slots, blocks[0, 0], panel_t, fetch_total
    )
    weight_pack = exchange_add(weight_pack, steps[1])
    weight_pack, per_slot_t = lax.optimization_barrier((weight_pack, per_slot_t))
    per_slot = per_slot_t.transpose(0, 2, 1).reshape(row_count, picks_each, block_size, feat_width)
    returned = lax.all_to_all(per_slot, "row", split_axis=0, concat_axis=0, tiled=True)
    weight_pack = exchange_add(weight_pack, steps[2])
    weight_pack, returned = lax.optimization_barrier((weight_pack, returned))
    incoming = group_rows(
        asked_for.reshape(-1),
        returned.reshape(fetch_total, block_size, feat_width),
        owned_count,
    )
    incoming = incoming.reshape(node_count, feat_width)
    grad_feats = (
        jnp.einsum("nh,dh->nd", grad_round, w_self, preferred_element_type=jnp.float32) + incoming
    )
    for step in steps[3:]:
        weight_pack = exchange_add(weight_pack, step)
    factor = 1.0 / math.sqrt(node_count * row_count * col_count)
    grad_self = weight_pack[:feat_width] * factor
    grad_neigh = weight_pack[feat_width : 2 * feat_width] * factor
    grad_bias = weight_pack[2 * feat_width] * factor
    return (
        output.astype(jnp.bfloat16)[None],
        grad_feats.astype(jnp.bfloat16)[None],
        grad_self,
        grad_neigh,
        grad_bias,
    )


def solution(mesh):
    return jax.shard_map(
        on_device,
        mesh=mesh,
        in_specs=(
            P("col", "row", None),
            P(),
            P(),
            P(),
            P("row", "col", None, None, None),
            P("row", "col", None),
            P("row", "col", None),
            P("row", "col", None),
            P("row", "col", None, None),
            P("col", "row", None),
        ),
        out_specs=(P("col", "row", None), P("col", "row", None), P(), P(), P()),
        check_vma=False,
    )
```

```python
import functools
import math

import jax
import jax.numpy as jnp
from jax import lax
from jax.experimental import pallas as pl
from jax.experimental.pallas import tpu as pltpu
from jax.sharding import PartitionSpec as P

GROUP = 32
DEGREE_ROWS = 16


def gelu_tanh(values):
    return jax.nn.gelu(values, approximate=True)


def select_rows(indices, table, total):
    picker = (indices[:, None] == jnp.arange(total, dtype=jnp.int32)[None, :]).astype(table.dtype)
    flat = table.reshape(total, -1)
    taken = jnp.dot(picker, flat, preferred_element_type=jnp.float32).astype(table.dtype)
    return taken.reshape((indices.shape[0],) + table.shape[1:])


def group_rows(indices, values, total):
    grouper = (jnp.arange(total, dtype=jnp.int32)[:, None] == indices[None, :]).astype(jnp.float32)
    flat = values.reshape(values.shape[0], -1)
    added = jnp.dot(
        grouper, flat, precision=lax.Precision.HIGHEST, preferred_element_type=jnp.float32
    )
    return added.reshape((total,) + values.shape[1:])


def _live_group(g, count_ref):
    return jnp.minimum(g, (count_ref[0] - 1) // GROUP)


def _forward_kernel(count_ref, row_ref, slot_ref, blk_ref, feat_ref, deg_ref, out_ref):
    g = pl.program_id(0)
    bs = blk_ref.shape[-1]
    node_count = out_ref.shape[1] - deg_ref.shape[1]
    owned = node_count // bs

    @pl.when(g == 0)
    def _():
        out_ref[:, :node_count, :] = jnp.zeros(
            (out_ref.shape[0], node_count, out_ref.shape[2]), jnp.float32
        )
        out_ref[:, node_count:, :] = deg_ref[...]

    count = count_ref[0]

    @pl.when(g * GROUP < count)
    def _():
        for j in range(GROUP):
            k = g * GROUP + j
            live = k < count
            r = row_ref[k]
            s = slot_ref[k]
            at = pl.multiple_of((r % owned) * bs, bs)
            prod = jnp.dot(blk_ref[j], feat_ref[s], preferred_element_type=jnp.float32)
            out_ref[r // owned, pl.ds(at, bs), :] += jnp.where(live, prod, 0.0)


def _backward_kernel(count_ref, row_ref, slot_ref, blk_ref, grad_ref, out_ref, gt_ref, acc_ref):
    g = pl.program_id(0)

    @pl.when(g == 0)
    def _():
        for r in range(grad_ref.shape[0]):
            gt_ref[r] = grad_ref[r].T
        acc_ref[...] = jnp.zeros_like(acc_ref)

    count = count_ref[0]

    @pl.when(g * GROUP < count)
    def _():
        for j in range(GROUP):
            k = g * GROUP + j
            live = k < count
            r = row_ref[k]
            s = slot_ref[k]
            prod = jnp.dot(gt_ref[r], blk_ref[j], preferred_element_type=jnp.float32)
            acc_ref[s] += jnp.where(live, prod, 0.0)

    @pl.when(g == pl.num_programs(0) - 1)
    def _():
        for s in range(out_ref.shape[0]):
            out_ref[s] = acc_ref[s].T


def aggregate_forward(counts, rows, slots, blocks, fetched, degree_rows, node_count):
    slot_total, bs, _ = blocks.shape
    fetch_total, _, width = fetched.shape
    chunks, pad, _ = degree_rows.shape
    out_rows = node_count + pad
    grid_spec = pltpu.PrefetchScalarGridSpec(
        num_scalar_prefetch=3,
        grid=(slot_total // GROUP,),
        in_specs=[
            pl.BlockSpec((GROUP, bs, bs), lambda g, c, r, s: (_live_group(g, c), 0, 0)),
            pl.BlockSpec((fetch_total, bs, width), lambda g, c, r, s: (0, 0, 0)),
            pl.BlockSpec((chunks, pad, width), lambda g, c, r, s: (0, 0, 0)),
        ],
        out_specs=pl.BlockSpec((chunks, out_rows, width), lambda g, c, r, s: (0, 0, 0)),
    )
    return pl.pallas_call(
        _forward_kernel,
        grid_spec=grid_spec,
        out_shape=jax.ShapeDtypeStruct((chunks, out_rows, width), jnp.float32),
        compiler_params=pltpu.CompilerParams(dimension_semantics=("arbitrary",)),
        cost_estimate=pl.CostEstimate(
            flops=2 * slot_total * bs * bs * width,
            bytes_accessed=blocks.size * 2 + fetched.size * 2 + chunks * out_rows * width * 4,
            transcendentals=0,
        ),
    )(counts, rows, slots, blocks, fetched, degree_rows)


def aggregate_backward(counts, rows, slots, blocks, grad_panel, fetch_total):
    slot_total, bs, _ = blocks.shape
    panel_blocks, _, width = grad_panel.shape
    grid_spec = pltpu.PrefetchScalarGridSpec(
        num_scalar_prefetch=3,
        grid=(slot_total // GROUP,),
        in_specs=[
            pl.BlockSpec((GROUP, bs, bs), lambda g, c, r, s: (_live_group(g, c), 0, 0)),
            pl.BlockSpec((panel_blocks, bs, width), lambda g, c, r, s: (0, 0, 0)),
        ],
        out_specs=pl.BlockSpec((fetch_total, bs, width), lambda g, c, r, s: (0, 0, 0)),
        scratch_shapes=[
            pltpu.VMEM((panel_blocks, width, bs), jnp.bfloat16),
            pltpu.VMEM((fetch_total, width, bs), jnp.float32),
        ],
    )
    return pl.pallas_call(
        _backward_kernel,
        grid_spec=grid_spec,
        out_shape=jax.ShapeDtypeStruct((fetch_total, bs, width), jnp.float32),
        compiler_params=pltpu.CompilerParams(dimension_semantics=("arbitrary",)),
        cost_estimate=pl.CostEstimate(
            flops=2 * slot_total * bs * bs * width,
            bytes_accessed=blocks.size * 2 + grad_panel.size * 2 + fetch_total * bs * width * 4,
            transcendentals=0,
        ),
    )(counts, rows, slots, blocks, grad_panel)


def exchange_steps(axes):
    steps = []
    for name in axes:
        size = lax.axis_size(name)
        step = 1
        while step < size:
            steps.append((name, size, step))
            step *= 2
    return steps[::-1]


def exchange_add(values, step):
    name, size, offset = step
    pairs = [(i, i ^ offset) for i in range(size)]
    return values + lax.ppermute(values, name, pairs)


def on_device(
    features, w_self, w_neigh, bias, blocks, blk_row, blk_slot, counts, col_list, cotangent
):
    own_feats = features[0]
    node_count, feat_width = own_feats.shape
    block_size = blocks.shape[-1]
    owned_count = node_count // block_size
    row_count = lax.axis_size("row")
    col_count = lax.axis_size("col")
    picks_each = col_list.shape[-1]
    fetch_total = row_count * picks_each
    panel_blocks = col_count * owned_count
    wanted = col_list[0, 0]
    asked_for = lax.all_to_all(wanted, "row", split_axis=0, concat_axis=0, tiled=True)
    block_rows = blk_row[0, 0]
    block_slots = blk_slot[0, 0]
    live_count = counts[0, 0]
    own_blocks = own_feats.reshape(owned_count, block_size, feat_width)
    outgoing = select_rows(asked_for.reshape(-1), own_blocks, owned_count)
    outgoing = outgoing.reshape(row_count, picks_each, block_size, feat_width)
    arrived = lax.all_to_all(outgoing, "row", split_axis=0, concat_axis=0, tiled=True)
    fetched = arrived.reshape(fetch_total, block_size, feat_width)
    adjacency = blocks[0, 0]
    live_rows = jnp.where(
        (jnp.arange(adjacency.shape[0]) < live_count[0])[:, None],
        jnp.sum(adjacency, axis=2, dtype=jnp.float32),
        0.0,
    )
    part_deg = group_rows(block_rows, live_rows, panel_blocks)
    part_deg = part_deg.reshape(col_count, owned_count, block_size)
    part_deg = jnp.pad(part_deg, ((0, 0), (0, DEGREE_ROWS - owned_count), (0, 0)))
    packed = aggregate_forward(
        live_count, block_rows, block_slots, adjacency, fetched, part_deg, node_count
    )
    packed = packed.reshape(col_count * (node_count + DEGREE_ROWS), feat_width)
    reduced = lax.psum_scatter(packed, "col", scatter_dimension=0, tiled=True)
    summed = reduced[:node_count]
    degree = reduced[node_count : node_count + owned_count].reshape(node_count)
    divisor = 1.0 + degree
    neighbors = (summed / divisor[:, None]).astype(jnp.bfloat16)
    hidden = (
        jnp.dot(own_feats, w_self, preferred_element_type=jnp.float32)
        + jnp.dot(neighbors, w_neigh, preferred_element_type=jnp.float32)
        + bias
    )
    output, pullback = jax.vjp(gelu_tanh, hidden)
    grad_hidden = pullback(cotangent[0].astype(jnp.float32))[0]
    grad_round = grad_hidden.astype(jnp.bfloat16)
    local_self = jnp.einsum("nd,nh->dh", own_feats, grad_round, preferred_element_type=jnp.float32)
    local_neigh = jnp.einsum("nd,nh->dh", neighbors, grad_round, preferred_element_type=jnp.float32)
    local_bias = jnp.sum(grad_round.astype(jnp.float32), axis=0)
    hid = local_bias.shape[0]
    weight_pack = jnp.concatenate(
        [local_self, local_neigh, jnp.broadcast_to(local_bias[None], (8, hid))], axis=0
    )
    steps = exchange_steps(("col", "row"))
    grad_agg = (
        jnp.einsum("nh,dh->nd", grad_round, w_neigh, preferred_element_type=jnp.float32)
        / divisor[:, None]
    )
    grad_agg = grad_agg.astype(jnp.bfloat16)
    adjoint_panel = lax.all_gather(grad_agg, "col", axis=0, tiled=True)
    weight_pack = exchange_add(weight_pack, steps[0])
    weight_pack, adjoint_panel = lax.optimization_barrier((weight_pack, adjoint_panel))
    per_slot = aggregate_backward(
        live_count,
        block_rows,
        block_slots,
        adjacency,
        adjoint_panel.reshape(panel_blocks, block_size, feat_width),
        fetch_total,
    )
    weight_pack = exchange_add(weight_pack, steps[1])
    weight_pack, per_slot = lax.optimization_barrier((weight_pack, per_slot))
    per_slot = per_slot.reshape(row_count, picks_each, block_size, feat_width)
    returned = lax.all_to_all(per_slot, "row", split_axis=0, concat_axis=0, tiled=True)
    weight_pack = exchange_add(weight_pack, steps[2])
    weight_pack, returned = lax.optimization_barrier((weight_pack, returned))
    incoming = group_rows(
        asked_for.reshape(-1),
        returned.reshape(fetch_total, block_size, feat_width),
        owned_count,
    )
    incoming = incoming.reshape(node_count, feat_width)
    grad_feats = (
        jnp.einsum("nh,dh->nd", grad_round, w_self, preferred_element_type=jnp.float32) + incoming
    )
    for step in steps[3:]:
        weight_pack = exchange_add(weight_pack, step)
    factor = 1.0 / math.sqrt(node_count * row_count * col_count)
    grad_self = weight_pack[:feat_width] * factor
    grad_neigh = weight_pack[feat_width : 2 * feat_width] * factor
    grad_bias = weight_pack[2 * feat_width] * factor
    return (
        output.astype(jnp.bfloat16)[None],
        grad_feats.astype(jnp.bfloat16)[None],
        grad_self,
        grad_neigh,
        grad_bias,
    )


def solution(mesh):
    return jax.shard_map(
        on_device,
        mesh=mesh,
        in_specs=(
            P("col", "row", None),
            P(),
            P(),
            P(),
            P("row", "col", None, None, None),
            P("row", "col", None),
            P("row", "col", None),
            P("row", "col", None),
            P("row", "col", None, None),
            P("col", "row", None),
        ),
        out_specs=(P("col", "row", None), P("col", "row", None), P(), P(), P()),
        check_vma=False,
    )
```

```python
import functools
import math

import jax
import jax.numpy as jnp
from jax import lax
from jax.experimental import pallas as pl
from jax.experimental.pallas import tpu as pltpu
from jax.sharding import PartitionSpec as P

GROUP = 32
DEGREE_ROWS = 16


def gelu_tanh(values):
    return jax.nn.gelu(values, approximate=True)


def select_rows(indices, table, total):
    picker = (indices[:, None] == jnp.arange(total, dtype=jnp.int32)[None, :]).astype(table.dtype)
    flat = table.reshape(total, -1)
    taken = jnp.dot(picker, flat, preferred_element_type=jnp.float32).astype(table.dtype)
    return taken.reshape((indices.shape[0],) + table.shape[1:])


def group_rows(indices, values, total):
    grouper = (jnp.arange(total, dtype=jnp.int32)[:, None] == indices[None, :]).astype(jnp.float32)
    flat = values.reshape(values.shape[0], -1)
    added = jnp.dot(
        grouper, flat, precision=lax.Precision.HIGHEST, preferred_element_type=jnp.float32
    )
    return added.reshape((total,) + values.shape[1:])


def _live_group(g, count_ref):
    return jnp.minimum(g, (count_ref[0] - 1) // GROUP)


def _forward_kernel(count_ref, row_ref, slot_ref, blk_ref, feat_ref, deg_ref, out_ref):
    g = pl.program_id(0)
    bs = blk_ref.shape[-1]
    node_count = out_ref.shape[1] - deg_ref.shape[1]
    owned = node_count // bs

    @pl.when(g == 0)
    def _():
        out_ref[:, :node_count, :] = jnp.zeros(
            (out_ref.shape[0], node_count, out_ref.shape[2]), jnp.float32
        )
        out_ref[:, node_count:, :] = deg_ref[...]

    count = count_ref[0]

    @pl.when(g * GROUP < count)
    def _():
        for j in range(GROUP):
            k = g * GROUP + j
            live = k < count
            r = row_ref[k]
            s = slot_ref[k]
            at = pl.multiple_of((r % owned) * bs, bs)
            prod = jnp.dot(blk_ref[j], feat_ref[s], preferred_element_type=jnp.float32)
            out_ref[r // owned, pl.ds(at, bs), :] += jnp.where(live, prod, 0.0)


def _backward_kernel(
    first, count_ref, row_ref, slot_ref, blk_ref, grad_ref, prev_ref, out_ref, gt_ref, acc_ref
):
    g = pl.program_id(0) + first

    @pl.when(pl.program_id(0) == 0)
    def _():
        for r in range(grad_ref.shape[0]):
            gt_ref[r] = grad_ref[r].T
        acc_ref[...] = jnp.zeros_like(acc_ref)

    count = count_ref[0]

    @pl.when(g * GROUP < count)
    def _():
        for j in range(GROUP):
            k = g * GROUP + j
            live = k < count
            r = row_ref[k]
            s = slot_ref[k]
            prod = jnp.dot(gt_ref[r], blk_ref[j], preferred_element_type=jnp.float32)
            acc_ref[s] += jnp.where(live, prod, 0.0)

    @pl.when(pl.program_id(0) == pl.num_programs(0) - 1)
    def _():
        for s in range(out_ref.shape[0]):
            out_ref[s] = acc_ref[s].T + prev_ref[s]


def aggregate_forward(counts, rows, slots, blocks, fetched, degree_rows, node_count):
    slot_total, bs, _ = blocks.shape
    fetch_total, _, width = fetched.shape
    chunks, pad, _ = degree_rows.shape
    out_rows = node_count + pad
    grid_spec = pltpu.PrefetchScalarGridSpec(
        num_scalar_prefetch=3,
        grid=(slot_total // GROUP,),
        in_specs=[
            pl.BlockSpec((GROUP, bs, bs), lambda g, c, r, s: (_live_group(g, c), 0, 0)),
            pl.BlockSpec((fetch_total, bs, width), lambda g, c, r, s: (0, 0, 0)),
            pl.BlockSpec((chunks, pad, width), lambda g, c, r, s: (0, 0, 0)),
        ],
        out_specs=pl.BlockSpec((chunks, out_rows, width), lambda g, c, r, s: (0, 0, 0)),
    )
    return pl.pallas_call(
        _forward_kernel,
        grid_spec=grid_spec,
        out_shape=jax.ShapeDtypeStruct((chunks, out_rows, width), jnp.float32),
        compiler_params=pltpu.CompilerParams(dimension_semantics=("arbitrary",)),
        cost_estimate=pl.CostEstimate(
            flops=2 * slot_total * bs * bs * width,
            bytes_accessed=blocks.size * 2 + fetched.size * 2 + chunks * out_rows * width * 4,
            transcendentals=0,
        ),
    )(counts, rows, slots, blocks, fetched, degree_rows)


def aggregate_backward(counts, rows, slots, blocks, grad_panel, previous, first, last):
    slot_total, bs, _ = blocks.shape
    panel_blocks, _, width = grad_panel.shape
    fetch_total = previous.shape[0]

    def block_at(g, c, r, s):
        return (_live_group(g + first, c), 0, 0)

    grid_spec = pltpu.PrefetchScalarGridSpec(
        num_scalar_prefetch=3,
        grid=(last - first,),
        in_specs=[
            pl.BlockSpec((GROUP, bs, bs), block_at),
            pl.BlockSpec((panel_blocks, bs, width), lambda g, c, r, s: (0, 0, 0)),
            pl.BlockSpec((fetch_total, bs, width), lambda g, c, r, s: (0, 0, 0)),
        ],
        out_specs=pl.BlockSpec((fetch_total, bs, width), lambda g, c, r, s: (0, 0, 0)),
        scratch_shapes=[
            pltpu.VMEM((panel_blocks, width, bs), jnp.bfloat16),
            pltpu.VMEM((fetch_total, width, bs), jnp.float32),
        ],
    )
    share = (last - first) * GROUP
    return pl.pallas_call(
        functools.partial(_backward_kernel, first),
        grid_spec=grid_spec,
        out_shape=jax.ShapeDtypeStruct((fetch_total, bs, width), jnp.float32),
        compiler_params=pltpu.CompilerParams(dimension_semantics=("arbitrary",)),
        cost_estimate=pl.CostEstimate(
            flops=2 * share * bs * bs * width,
            bytes_accessed=share * bs * bs * 2 + grad_panel.size * 2 + fetch_total * bs * width * 8,
            transcendentals=0,
        ),
    )(counts, rows, slots, blocks, grad_panel, previous)


def exchange_steps(axes):
    steps = []
    for name in axes:
        size = lax.axis_size(name)
        step = 1
        while step < size:
            steps.append((name, size, step))
            step *= 2
    return steps[::-1]


def exchange_add(values, step):
    name, size, offset = step
    pairs = [(i, i ^ offset) for i in range(size)]
    return values + lax.ppermute(values, name, pairs)


def on_device(
    features, w_self, w_neigh, bias, blocks, blk_row, blk_slot, counts, col_list, cotangent
):
    own_feats = features[0]
    node_count, feat_width = own_feats.shape
    block_size = blocks.shape[-1]
    owned_count = node_count // block_size
    row_count = lax.axis_size("row")
    col_count = lax.axis_size("col")
    picks_each = col_list.shape[-1]
    fetch_total = row_count * picks_each
    panel_blocks = col_count * owned_count
    wanted = col_list[0, 0]
    asked_for = lax.all_to_all(wanted, "row", split_axis=0, concat_axis=0, tiled=True)
    block_rows = blk_row[0, 0]
    block_slots = blk_slot[0, 0]
    live_count = counts[0, 0]
    own_blocks = own_feats.reshape(owned_count, block_size, feat_width)
    outgoing = select_rows(asked_for.reshape(-1), own_blocks, owned_count)
    outgoing = outgoing.reshape(row_count, picks_each, block_size, feat_width)
    arrived = lax.all_to_all(outgoing, "row", split_axis=0, concat_axis=0, tiled=True)
    fetched = arrived.reshape(fetch_total, block_size, feat_width)
    adjacency = blocks[0, 0]
    live_rows = jnp.where(
        (jnp.arange(adjacency.shape[0]) < live_count[0])[:, None],
        jnp.sum(adjacency, axis=2, dtype=jnp.float32),
        0.0,
    )
    part_deg = group_rows(block_rows, live_rows, panel_blocks)
    part_deg = part_deg.reshape(col_count, owned_count, block_size)
    part_deg = jnp.pad(part_deg, ((0, 0), (0, DEGREE_ROWS - owned_count), (0, 0)))
    packed = aggregate_forward(
        live_count, block_rows, block_slots, adjacency, fetched, part_deg, node_count
    )
    packed = packed.reshape(col_count * (node_count + DEGREE_ROWS), feat_width)
    reduced = lax.psum_scatter(packed, "col", scatter_dimension=0, tiled=True)
    summed = reduced[:node_count]
    degree = reduced[node_count : node_count + owned_count].reshape(node_count)
    divisor = 1.0 + degree
    neighbors = (summed / divisor[:, None]).astype(jnp.bfloat16)
    hidden = (
        jnp.dot(own_feats, w_self, preferred_element_type=jnp.float32)
        + jnp.dot(neighbors, w_neigh, preferred_element_type=jnp.float32)
        + bias
    )
    output, pullback = jax.vjp(gelu_tanh, hidden)
    grad_hidden = pullback(cotangent[0].astype(jnp.float32))[0]
    grad_round = grad_hidden.astype(jnp.bfloat16)
    local_self = jnp.einsum("nd,nh->dh", own_feats, grad_round, preferred_element_type=jnp.float32)
    local_neigh = jnp.einsum("nd,nh->dh", neighbors, grad_round, preferred_element_type=jnp.float32)
    local_bias = jnp.sum(grad_round.astype(jnp.float32), axis=0)
    hid = local_bias.shape[0]
    weight_pack = jnp.concatenate(
        [local_self, local_neigh, jnp.broadcast_to(local_bias[None], (8, hid))], axis=0
    )
    steps = exchange_steps(("col", "row"))
    cross_step = [step for step in steps if step[0] == "col"][0]
    grad_agg = (
        jnp.einsum("nh,dh->nd", grad_round, w_neigh, preferred_element_type=jnp.float32)
        / divisor[:, None]
    )
    grad_agg = grad_agg.astype(jnp.bfloat16)
    adjoint_panel = lax.all_gather(grad_agg, "col", axis=0, tiled=True)
    weight_pack = exchange_add(weight_pack, steps[0])
    weight_pack, adjoint_panel = lax.optimization_barrier((weight_pack, adjoint_panel))
    panel = adjoint_panel.reshape(panel_blocks, block_size, feat_width)
    groups = adjacency.shape[0] // GROUP
    half = groups // 2
    per_slot = jnp.zeros((fetch_total, block_size, feat_width), jnp.float32)
    per_slot = aggregate_backward(
        live_count, block_rows, block_slots, adjacency, panel, per_slot, 0, half
    )
    weight_pack = exchange_add(weight_pack, steps[1])
    weight_pack, per_slot = lax.optimization_barrier((weight_pack, per_slot))
    per_slot = aggregate_backward(
        live_count, block_rows, block_slots, adjacency, panel, per_slot, half, groups
    )
    weight_pack = exchange_add(weight_pack, steps[2])
    weight_pack, per_slot = lax.optimization_barrier((weight_pack, per_slot))
    per_slot = per_slot.reshape(row_count, picks_each, block_size, feat_width)
    returned = lax.all_to_all(per_slot, "row", split_axis=0, concat_axis=0, tiled=True)
    weight_pack = exchange_add(weight_pack, cross_step)
    weight_pack, returned = lax.optimization_barrier((weight_pack, returned))
    incoming = group_rows(
        asked_for.reshape(-1),
        returned.reshape(fetch_total, block_size, feat_width),
        owned_count,
    )
    incoming = incoming.reshape(node_count, feat_width)
    grad_feats = (
        jnp.einsum("nh,dh->nd", grad_round, w_self, preferred_element_type=jnp.float32) + incoming
    )
    for step in steps[3:]:
        if step != cross_step:
            weight_pack = exchange_add(weight_pack, step)
    factor = 1.0 / math.sqrt(node_count * row_count * col_count)
    grad_self = weight_pack[:feat_width] * factor
    grad_neigh = weight_pack[feat_width : 2 * feat_width] * factor
    grad_bias = weight_pack[2 * feat_width] * factor
    return (
        output.astype(jnp.bfloat16)[None],
        grad_feats.astype(jnp.bfloat16)[None],
        grad_self,
        grad_neigh,
        grad_bias,
    )


def solution(mesh):
    return jax.shard_map(
        on_device,
        mesh=mesh,
        in_specs=(
            P("col", "row", None),
            P(),
            P(),
            P(),
            P("row", "col", None, None, None),
            P("row", "col", None),
            P("row", "col", None),
            P("row", "col", None),
            P("row", "col", None, None),
            P("col", "row", None),
        ),
        out_specs=(P("col", "row", None), P("col", "row", None), P(), P(), P()),
        check_vma=False,
    )
```

```python
import functools
import math

import jax
import jax.numpy as jnp
from jax import lax
from jax.experimental import pallas as pl
from jax.experimental.pallas import tpu as pltpu
from jax.sharding import PartitionSpec as P


GROUP = 32
DEGREE_ROWS = 16


def gelu_tanh(values):
    return jax.nn.gelu(values, approximate=True)


def select_rows(indices, table, total):
    picker = (indices[:, None] == jnp.arange(total, dtype=jnp.int32)[None, :]).astype(table.dtype)
    flat = table.reshape(total, -1)
    taken = jnp.dot(picker, flat, preferred_element_type=jnp.float32).astype(table.dtype)
    return taken.reshape((indices.shape[0],) + table.shape[1:])


def group_rows(indices, values, total):
    grouper = (jnp.arange(total, dtype=jnp.int32)[:, None] == indices[None, :]).astype(jnp.float32)
    flat = values.reshape(values.shape[0], -1)
    added = jnp.dot(
        grouper, flat, precision=lax.Precision.HIGHEST, preferred_element_type=jnp.float32
    )
    return added.reshape((total,) + values.shape[1:])


def _live_group(g, count_ref):
    return jnp.minimum(g, (count_ref[0] - 1) // GROUP)


def _forward_kernel(count_ref, row_ref, slot_ref, blk_ref, feat_ref, deg_ref, out_ref):
    g = pl.program_id(0)
    bs = blk_ref.shape[-1]
    node_count = out_ref.shape[1] - deg_ref.shape[1]
    owned = node_count // bs

    @pl.when(g == 0)
    def _():
        out_ref[:, :node_count, :] = jnp.zeros(
            (out_ref.shape[0], node_count, out_ref.shape[2]), jnp.float32
        )
        out_ref[:, node_count:, :] = deg_ref[...]

    count = count_ref[0]

    @pl.when(g * GROUP < count)
    def _():
        for j in range(GROUP):
            k = g * GROUP + j
            live = k < count
            r = row_ref[k]
            s = slot_ref[k]
            at = pl.multiple_of((r % owned) * bs, bs)
            prod = jnp.dot(blk_ref[j], feat_ref[s], preferred_element_type=jnp.float32)
            out_ref[r // owned, pl.ds(at, bs), :] += jnp.where(live, prod, 0.0)


def _backward_kernel(
    first, count_ref, row_ref, slot_ref, blk_ref, grad_ref, prev_ref, out_ref, gt_ref, acc_ref
):
    g = pl.program_id(0) + first

    @pl.when(pl.program_id(0) == 0)
    def _():
        for r in range(grad_ref.shape[0]):
            gt_ref[r] = grad_ref[r].T
        acc_ref[...] = jnp.zeros_like(acc_ref)

    count = count_ref[0]

    @pl.when(g * GROUP < count)
    def _():
        for j in range(GROUP):
            k = g * GROUP + j
            live = k < count
            r = row_ref[k]
            s = slot_ref[k]
            prod = jnp.dot(gt_ref[r], blk_ref[j], preferred_element_type=jnp.float32)
            acc_ref[s] += jnp.where(live, prod, 0.0)

    @pl.when(pl.program_id(0) == pl.num_programs(0) - 1)
    def _():
        for s in range(out_ref.shape[0]):
            out_ref[s] = acc_ref[s].T + prev_ref[s]


def aggregate_forward(counts, rows, slots, blocks, fetched, degree_rows, node_count):
    slot_total, bs, _ = blocks.shape
    fetch_total, _, width = fetched.shape
    chunks, pad, _ = degree_rows.shape
    out_rows = node_count + pad
    grid_spec = pltpu.PrefetchScalarGridSpec(
        num_scalar_prefetch=3,
        grid=(slot_total // GROUP,),
        in_specs=[
            pl.BlockSpec((GROUP, bs, bs), lambda g, c, r, s: (_live_group(g, c), 0, 0)),
            pl.BlockSpec((fetch_total, bs, width), lambda g, c, r, s: (0, 0, 0)),
            pl.BlockSpec((chunks, pad, width), lambda g, c, r, s: (0, 0, 0)),
        ],
        out_specs=pl.BlockSpec((chunks, out_rows, width), lambda g, c, r, s: (0, 0, 0)),
    )
    return pl.pallas_call(
        _forward_kernel,
        grid_spec=grid_spec,
        out_shape=jax.ShapeDtypeStruct((chunks, out_rows, width), jnp.float32),
        compiler_params=pltpu.CompilerParams(dimension_semantics=("arbitrary",)),
        cost_estimate=pl.CostEstimate(
            flops=2 * slot_total * bs * bs * width,
            bytes_accessed=blocks.size * 2 + fetched.size * 2 + chunks * out_rows * width * 4,
            transcendentals=0,
        ),
    )(counts, rows, slots, blocks, fetched, degree_rows)


def aggregate_backward(counts, rows, slots, blocks, grad_panel, previous, first, last):
    slot_total, bs, _ = blocks.shape
    panel_blocks, _, width = grad_panel.shape
    fetch_total = previous.shape[0]

    def block_at(g, c, r, s):
        return (_live_group(g + first, c), 0, 0)

    grid_spec = pltpu.PrefetchScalarGridSpec(
        num_scalar_prefetch=3,
        grid=(last - first,),
        in_specs=[
            pl.BlockSpec((GROUP, bs, bs), block_at),
            pl.BlockSpec((panel_blocks, bs, width), lambda g, c, r, s: (0, 0, 0)),
            pl.BlockSpec((fetch_total, bs, width), lambda g, c, r, s: (0, 0, 0)),
        ],
        out_specs=pl.BlockSpec((fetch_total, bs, width), lambda g, c, r, s: (0, 0, 0)),
        scratch_shapes=[
            pltpu.VMEM((panel_blocks, width, bs), jnp.bfloat16),
            pltpu.VMEM((fetch_total, width, bs), jnp.float32),
        ],
    )
    share = (last - first) * GROUP
    return pl.pallas_call(
        functools.partial(_backward_kernel, first),
        grid_spec=grid_spec,
        out_shape=jax.ShapeDtypeStruct((fetch_total, bs, width), jnp.float32),
        compiler_params=pltpu.CompilerParams(dimension_semantics=("arbitrary",)),
        cost_estimate=pl.CostEstimate(
            flops=2 * share * bs * bs * width,
            bytes_accessed=share * bs * bs * 2 + grad_panel.size * 2 + fetch_total * bs * width * 8,
            transcendentals=0,
        ),
    )(counts, rows, slots, blocks, grad_panel, previous)


def exchange_steps(axes):
    steps = []
    for name in axes:
        size = lax.axis_size(name)
        step = 1
        while step < size:
            steps.append((name, size, step))
            step *= 2
    return steps[::-1]


def spread(chunks, name):
    size = lax.axis_size(name)
    me = lax.axis_index(name)
    received = [chunks[me]]
    for offset in range(1, size):
        pairs = [(i, (i + offset) % size) for i in range(size)]
        received.append(lax.ppermute(chunks[(me + offset) % size], name, pairs))
    return jnp.stack(received)


def spread_sources(name):
    size = lax.axis_size(name)
    me = lax.axis_index(name)
    return (me - jnp.arange(size, dtype=jnp.int32)) % size


def exchange_add(values, step):
    name, size, offset = step
    pairs = [(i, i ^ offset) for i in range(size)]
    return values + lax.ppermute(values, name, pairs)


def on_device(
    features, w_self, w_neigh, bias, blocks, blk_row, blk_slot, counts, col_list, cotangent
):
    own_feats = features[0]
    node_count, feat_width = own_feats.shape
    block_size = blocks.shape[-1]
    owned_count = node_count // block_size
    row_count = lax.axis_size("row")
    col_count = lax.axis_size("col")
    picks_each = col_list.shape[-1]
    fetch_total = row_count * picks_each
    panel_blocks = col_count * owned_count
    wanted = col_list[0, 0]
    asked_for = lax.all_to_all(wanted, "row", split_axis=0, concat_axis=0, tiled=True)
    block_rows = blk_row[0, 0]
    block_slots = blk_slot[0, 0]
    live_count = counts[0, 0]
    own_blocks = own_feats.reshape(owned_count, block_size, feat_width)
    outgoing = select_rows(asked_for.reshape(-1), own_blocks, owned_count)
    outgoing = outgoing.reshape(row_count, picks_each, block_size, feat_width)
    arrived = lax.all_to_all(outgoing, "row", split_axis=0, concat_axis=0, tiled=True)
    fetched = arrived.reshape(fetch_total, block_size, feat_width)
    adjacency = blocks[0, 0]
    live_rows = jnp.where(
        (jnp.arange(adjacency.shape[0]) < live_count[0])[:, None],
        jnp.sum(adjacency, axis=2, dtype=jnp.float32),
        0.0,
    )
    part_deg = group_rows(block_rows, live_rows, panel_blocks)
    part_deg = part_deg.reshape(col_count, owned_count, block_size)
    part_deg = jnp.pad(part_deg, ((0, 0), (0, DEGREE_ROWS - owned_count), (0, 0)))
    packed = aggregate_forward(
        live_count, block_rows, block_slots, adjacency, fetched, part_deg, node_count
    )
    packed = packed.reshape(col_count * (node_count + DEGREE_ROWS), feat_width)
    reduced = lax.psum_scatter(packed, "col", scatter_dimension=0, tiled=True)
    summed = reduced[:node_count]
    degree = reduced[node_count : node_count + owned_count].reshape(node_count)
    divisor = 1.0 + degree
    neighbors = (summed / divisor[:, None]).astype(jnp.bfloat16)
    hidden = (
        jnp.dot(own_feats, w_self, preferred_element_type=jnp.float32)
        + jnp.dot(neighbors, w_neigh, preferred_element_type=jnp.float32)
        + bias
    )
    output, pullback = jax.vjp(gelu_tanh, hidden)
    grad_hidden = pullback(cotangent[0].astype(jnp.float32))[0]
    grad_round = grad_hidden.astype(jnp.bfloat16)
    local_self = jnp.einsum("nd,nh->dh", own_feats, grad_round, preferred_element_type=jnp.float32)
    local_neigh = jnp.einsum("nd,nh->dh", neighbors, grad_round, preferred_element_type=jnp.float32)
    local_bias = jnp.sum(grad_round.astype(jnp.float32), axis=0)
    hid = local_bias.shape[0]
    weight_pack = jnp.concatenate(
        [local_self, local_neigh, jnp.broadcast_to(local_bias[None], (8, hid))], axis=0
    )
    steps = exchange_steps(("col", "row"))
    cross_step = [step for step in steps if step[0] == "col"][0]
    grad_agg = (
        jnp.einsum("nh,dh->nd", grad_round, w_neigh, preferred_element_type=jnp.float32)
        / divisor[:, None]
    )
    grad_agg = grad_agg.astype(jnp.bfloat16)
    adjoint_panel = lax.all_gather(grad_agg, "col", axis=0, tiled=True)
    weight_pack = exchange_add(weight_pack, steps[0])
    weight_pack, adjoint_panel = lax.optimization_barrier((weight_pack, adjoint_panel))
    panel = adjoint_panel.reshape(panel_blocks, block_size, feat_width)
    groups = adjacency.shape[0] // GROUP
    half = groups // 2
    per_slot = jnp.zeros((fetch_total, block_size, feat_width), jnp.float32)
    per_slot = aggregate_backward(
        live_count, block_rows, block_slots, adjacency, panel, per_slot, 0, half
    )
    weight_pack = exchange_add(weight_pack, steps[1])
    weight_pack, per_slot = lax.optimization_barrier((weight_pack, per_slot))
    per_slot = aggregate_backward(
        live_count, block_rows, block_slots, adjacency, panel, per_slot, half, groups
    )
    weight_pack = exchange_add(weight_pack, steps[2])
    weight_pack, per_slot = lax.optimization_barrier((weight_pack, per_slot))
    per_slot = per_slot.reshape(row_count, picks_each, block_size, feat_width)
    returned = spread(per_slot, "row")
    weight_pack = exchange_add(weight_pack, cross_step)
    weight_pack, returned = lax.optimization_barrier((weight_pack, returned))
    incoming = group_rows(
        asked_for[spread_sources("row")].reshape(-1),
        returned.reshape(fetch_total, block_size, feat_width),
        owned_count,
    )
    incoming = incoming.reshape(node_count, feat_width)
    grad_feats = (
        jnp.einsum("nh,dh->nd", grad_round, w_self, preferred_element_type=jnp.float32) + incoming
    )
    for step in steps[3:]:
        if step != cross_step:
            weight_pack = exchange_add(weight_pack, step)
    factor = 1.0 / math.sqrt(node_count * row_count * col_count)
    grad_self = weight_pack[:feat_width] * factor
    grad_neigh = weight_pack[feat_width : 2 * feat_width] * factor
    grad_bias = weight_pack[2 * feat_width] * factor
    return (
        output.astype(jnp.bfloat16)[None],
        grad_feats.astype(jnp.bfloat16)[None],
        grad_self,
        grad_neigh,
        grad_bias,
    )


def solution(mesh):
    return jax.shard_map(
        on_device,
        mesh=mesh,
        in_specs=(
            P("col", "row", None),
            P(),
            P(),
            P(),
            P("row", "col", None, None, None),
            P("row", "col", None),
            P("row", "col", None),
            P("row", "col", None),
            P("row", "col", None, None),
            P("col", "row", None),
        ),
        out_specs=(P("col", "row", None), P("col", "row", None), P(), P(), P()),
        check_vma=False,
    )
```

```python
import functools
import math

import jax
import jax.numpy as jnp
from jax import lax
from jax.experimental import pallas as pl
from jax.experimental.pallas import tpu as pltpu
from jax.sharding import PartitionSpec as P


GROUP = 32
DEGREE_ROWS = 16


def gelu_tanh(values):
    return jax.nn.gelu(values, approximate=True)


def select_rows(indices, table, total):
    picker = (indices[:, None] == jnp.arange(total, dtype=jnp.int32)[None, :]).astype(table.dtype)
    flat = table.reshape(total, -1)
    taken = jnp.dot(picker, flat, preferred_element_type=jnp.float32).astype(table.dtype)
    return taken.reshape((indices.shape[0],) + table.shape[1:])


def group_rows(indices, values, total):
    grouper = (jnp.arange(total, dtype=jnp.int32)[:, None] == indices[None, :]).astype(jnp.float32)
    flat = values.reshape(values.shape[0], -1)
    added = jnp.dot(
        grouper, flat, precision=lax.Precision.HIGHEST, preferred_element_type=jnp.float32
    )
    return added.reshape((total,) + values.shape[1:])


def _live_group(g, count_ref):
    return jnp.minimum(g, (count_ref[0] - 1) // GROUP)


def _forward_kernel(count_ref, row_ref, slot_ref, blk_ref, feat_ref, deg_ref, out_ref):
    g = pl.program_id(0)
    bs = blk_ref.shape[-1]
    node_count = out_ref.shape[1] - deg_ref.shape[1]
    owned = node_count // bs

    @pl.when(g == 0)
    def _():
        out_ref[:, :node_count, :] = jnp.zeros(
            (out_ref.shape[0], node_count, out_ref.shape[2]), jnp.float32
        )
        out_ref[:, node_count:, :] = deg_ref[...]

    count = count_ref[0]

    @pl.when(g * GROUP < count)
    def _():
        for j in range(GROUP):
            k = g * GROUP + j
            live = k < count
            r = row_ref[k]
            s = slot_ref[k]
            at = pl.multiple_of((r % owned) * bs, bs)
            prod = jnp.dot(blk_ref[j], feat_ref[s], preferred_element_type=jnp.float32)
            out_ref[r // owned, pl.ds(at, bs), :] += jnp.where(live, prod, 0.0)


def _backward_kernel(
    first, count_ref, row_ref, slot_ref, blk_ref, grad_ref, prev_ref, out_ref, gt_ref, acc_ref
):
    g = pl.program_id(0) + first

    @pl.when(pl.program_id(0) == 0)
    def _():
        for r in range(grad_ref.shape[0]):
            gt_ref[r] = grad_ref[r].T
        acc_ref[...] = jnp.zeros_like(acc_ref)

    count = count_ref[0]

    @pl.when(g * GROUP < count)
    def _():
        for j in range(GROUP):
            k = g * GROUP + j
            live = k < count
            r = row_ref[k]
            s = slot_ref[k]
            prod = jnp.dot(gt_ref[r], blk_ref[j], preferred_element_type=jnp.float32)
            acc_ref[s] += jnp.where(live, prod, 0.0)

    @pl.when(pl.program_id(0) == pl.num_programs(0) - 1)
    def _():
        for s in range(out_ref.shape[0]):
            out_ref[s] = acc_ref[s].T + prev_ref[s]


def aggregate_forward(counts, rows, slots, blocks, fetched, degree_rows, node_count):
    slot_total, bs, _ = blocks.shape
    fetch_total, _, width = fetched.shape
    chunks, pad, _ = degree_rows.shape
    out_rows = node_count + pad
    grid_spec = pltpu.PrefetchScalarGridSpec(
        num_scalar_prefetch=3,
        grid=(slot_total // GROUP,),
        in_specs=[
            pl.BlockSpec((GROUP, bs, bs), lambda g, c, r, s: (_live_group(g, c), 0, 0)),
            pl.BlockSpec((fetch_total, bs, width), lambda g, c, r, s: (0, 0, 0)),
            pl.BlockSpec((chunks, pad, width), lambda g, c, r, s: (0, 0, 0)),
        ],
        out_specs=pl.BlockSpec((chunks, out_rows, width), lambda g, c, r, s: (0, 0, 0)),
    )
    return pl.pallas_call(
        _forward_kernel,
        grid_spec=grid_spec,
        out_shape=jax.ShapeDtypeStruct((chunks, out_rows, width), jnp.float32),
        compiler_params=pltpu.CompilerParams(dimension_semantics=("arbitrary",)),
        cost_estimate=pl.CostEstimate(
            flops=2 * slot_total * bs * bs * width,
            bytes_accessed=blocks.size * 2 + fetched.size * 2 + chunks * out_rows * width * 4,
            transcendentals=0,
        ),
    )(counts, rows, slots, blocks, fetched, degree_rows)


def aggregate_backward(counts, rows, slots, blocks, grad_panel, previous, first, last):
    slot_total, bs, _ = blocks.shape
    panel_blocks, _, width = grad_panel.shape
    fetch_total = previous.shape[0]

    def block_at(g, c, r, s):
        return (_live_group(g + first, c), 0, 0)

    grid_spec = pltpu.PrefetchScalarGridSpec(
        num_scalar_prefetch=3,
        grid=(last - first,),
        in_specs=[
            pl.BlockSpec((GROUP, bs, bs), block_at),
            pl.BlockSpec((panel_blocks, bs, width), lambda g, c, r, s: (0, 0, 0)),
            pl.BlockSpec((fetch_total, bs, width), lambda g, c, r, s: (0, 0, 0)),
        ],
        out_specs=pl.BlockSpec((fetch_total, bs, width), lambda g, c, r, s: (0, 0, 0)),
        scratch_shapes=[
            pltpu.VMEM((panel_blocks, width, bs), jnp.bfloat16),
            pltpu.VMEM((fetch_total, width, bs), jnp.float32),
        ],
    )
    share = (last - first) * GROUP
    return pl.pallas_call(
        functools.partial(_backward_kernel, first),
        grid_spec=grid_spec,
        out_shape=jax.ShapeDtypeStruct((fetch_total, bs, width), jnp.float32),
        compiler_params=pltpu.CompilerParams(dimension_semantics=("arbitrary",)),
        cost_estimate=pl.CostEstimate(
            flops=2 * share * bs * bs * width,
            bytes_accessed=share * bs * bs * 2 + grad_panel.size * 2 + fetch_total * bs * width * 8,
            transcendentals=0,
        ),
    )(counts, rows, slots, blocks, grad_panel, previous)


def exchange_steps(axes):
    steps = []
    for name in axes:
        size = lax.axis_size(name)
        step = 1
        while step < size:
            steps.append((name, size, step))
            step *= 2
    return steps[::-1]


def spread(chunks, name):
    size = lax.axis_size(name)
    me = lax.axis_index(name)
    received = [chunks[me]]
    for offset in range(1, size):
        pairs = [(i, (i + offset) % size) for i in range(size)]
        received.append(lax.ppermute(chunks[(me + offset) % size], name, pairs))
    return jnp.stack(received)


def scatter_sum(chunks, name):
    size = lax.axis_size(name)
    me = lax.axis_index(name)
    offset = 1
    while offset < size:
        mine = (me // offset) % 2
        paired = chunks.reshape((chunks.shape[0] // 2, 2) + chunks.shape[1:])
        keep = lax.dynamic_index_in_dim(paired, mine, axis=1, keepdims=False)
        send = lax.dynamic_index_in_dim(paired, 1 - mine, axis=1, keepdims=False)
        pairs = [(i, i ^ offset) for i in range(size)]
        chunks = keep + lax.ppermute(send, name, pairs)
        offset *= 2
    return chunks[0]


def spread_sources(name):
    size = lax.axis_size(name)
    me = lax.axis_index(name)
    return (me - jnp.arange(size, dtype=jnp.int32)) % size


def exchange_add(values, step):
    name, size, offset = step
    pairs = [(i, i ^ offset) for i in range(size)]
    return values + lax.ppermute(values, name, pairs)


def on_device(
    features, w_self, w_neigh, bias, blocks, blk_row, blk_slot, counts, col_list, cotangent
):
    own_feats = features[0]
    node_count, feat_width = own_feats.shape
    block_size = blocks.shape[-1]
    owned_count = node_count // block_size
    row_count = lax.axis_size("row")
    col_count = lax.axis_size("col")
    picks_each = col_list.shape[-1]
    fetch_total = row_count * picks_each
    panel_blocks = col_count * owned_count
    wanted = col_list[0, 0]
    asked_for = lax.all_to_all(wanted, "row", split_axis=0, concat_axis=0, tiled=True)
    block_rows = blk_row[0, 0]
    block_slots = blk_slot[0, 0]
    live_count = counts[0, 0]
    own_blocks = own_feats.reshape(owned_count, block_size, feat_width)
    outgoing = select_rows(asked_for.reshape(-1), own_blocks, owned_count)
    outgoing = outgoing.reshape(row_count, picks_each, block_size, feat_width)
    arrived = lax.all_to_all(outgoing, "row", split_axis=0, concat_axis=0, tiled=True)
    fetched = arrived.reshape(fetch_total, block_size, feat_width)
    adjacency = blocks[0, 0]
    live_rows = jnp.where(
        (jnp.arange(adjacency.shape[0]) < live_count[0])[:, None],
        jnp.sum(adjacency, axis=2, dtype=jnp.float32),
        0.0,
    )
    part_deg = group_rows(block_rows, live_rows, panel_blocks)
    part_deg = part_deg.reshape(col_count, owned_count, block_size)
    part_deg = jnp.pad(part_deg, ((0, 0), (0, DEGREE_ROWS - owned_count), (0, 0)))
    packed = aggregate_forward(
        live_count, block_rows, block_slots, adjacency, fetched, part_deg, node_count
    )
    reduced = scatter_sum(packed, "col")
    summed = reduced[:node_count]
    degree = reduced[node_count : node_count + owned_count].reshape(node_count)
    divisor = 1.0 + degree
    neighbors = (summed / divisor[:, None]).astype(jnp.bfloat16)
    hidden = (
        jnp.dot(own_feats, w_self, preferred_element_type=jnp.float32)
        + jnp.dot(neighbors, w_neigh, preferred_element_type=jnp.float32)
        + bias
    )
    output, pullback = jax.vjp(gelu_tanh, hidden)
    grad_hidden = pullback(cotangent[0].astype(jnp.float32))[0]
    grad_round = grad_hidden.astype(jnp.bfloat16)
    local_self = jnp.einsum("nd,nh->dh", own_feats, grad_round, preferred_element_type=jnp.float32)
    local_neigh = jnp.einsum("nd,nh->dh", neighbors, grad_round, preferred_element_type=jnp.float32)
    local_bias = jnp.sum(grad_round.astype(jnp.float32), axis=0)
    hid = local_bias.shape[0]
    weight_pack = jnp.concatenate(
        [local_self, local_neigh, jnp.broadcast_to(local_bias[None], (8, hid))], axis=0
    )
    steps = exchange_steps(("col", "row"))
    cross_step = [step for step in steps if step[0] == "col"][0]
    grad_agg = (
        jnp.einsum("nh,dh->nd", grad_round, w_neigh, preferred_element_type=jnp.float32)
        / divisor[:, None]
    )
    grad_agg = grad_agg.astype(jnp.bfloat16)
    adjoint_panel = lax.all_gather(grad_agg, "col", axis=0, tiled=True)
    weight_pack = exchange_add(weight_pack, steps[0])
    weight_pack, adjoint_panel = lax.optimization_barrier((weight_pack, adjoint_panel))
    panel = adjoint_panel.reshape(panel_blocks, block_size, feat_width)
    groups = adjacency.shape[0] // GROUP
    half = groups // 2
    per_slot = jnp.zeros((fetch_total, block_size, feat_width), jnp.float32)
    per_slot = aggregate_backward(
        live_count, block_rows, block_slots, adjacency, panel, per_slot, 0, half
    )
    weight_pack = exchange_add(weight_pack, steps[1])
    weight_pack, per_slot = lax.optimization_barrier((weight_pack, per_slot))
    per_slot = aggregate_backward(
        live_count, block_rows, block_slots, adjacency, panel, per_slot, half, groups
    )
    weight_pack = exchange_add(weight_pack, steps[2])
    weight_pack, per_slot = lax.optimization_barrier((weight_pack, per_slot))
    per_slot = per_slot.reshape(row_count, picks_each, block_size, feat_width)
    returned = spread(per_slot, "row")
    weight_pack = exchange_add(weight_pack, cross_step)
    weight_pack, returned = lax.optimization_barrier((weight_pack, returned))
    incoming = group_rows(
        asked_for[spread_sources("row")].reshape(-1),
        returned.reshape(fetch_total, block_size, feat_width),
        owned_count,
    )
    incoming = incoming.reshape(node_count, feat_width)
    grad_feats = (
        jnp.einsum("nh,dh->nd", grad_round, w_self, preferred_element_type=jnp.float32) + incoming
    )
    for step in steps[3:]:
        if step != cross_step:
            weight_pack = exchange_add(weight_pack, step)
    factor = 1.0 / math.sqrt(node_count * row_count * col_count)
    grad_self = weight_pack[:feat_width] * factor
    grad_neigh = weight_pack[feat_width : 2 * feat_width] * factor
    grad_bias = weight_pack[2 * feat_width] * factor
    return (
        output.astype(jnp.bfloat16)[None],
        grad_feats.astype(jnp.bfloat16)[None],
        grad_self,
        grad_neigh,
        grad_bias,
    )


def solution(mesh):
    return jax.shard_map(
        on_device,
        mesh=mesh,
        in_specs=(
            P("col", "row", None),
            P(),
            P(),
            P(),
            P("row", "col", None, None, None),
            P("row", "col", None),
            P("row", "col", None),
            P("row", "col", None),
            P("row", "col", None, None),
            P("col", "row", None),
        ),
        out_specs=(P("col", "row", None), P("col", "row", None), P(), P(), P()),
        check_vma=False,
    )
```

```python
import functools
import math

import jax
import jax.numpy as jnp
from jax import lax
from jax.experimental import pallas as pl
from jax.experimental.pallas import tpu as pltpu
from jax.sharding import PartitionSpec as P


GROUP = 32
DEGREE_ROWS = 16


def gelu_tanh(values):
    return jax.nn.gelu(values, approximate=True)


def select_rows(indices, table, total):
    picker = (indices[:, None] == jnp.arange(total, dtype=jnp.int32)[None, :]).astype(table.dtype)
    flat = table.reshape(total, -1)
    taken = jnp.dot(picker, flat, preferred_element_type=jnp.float32).astype(table.dtype)
    return taken.reshape((indices.shape[0],) + table.shape[1:])


def group_rows(indices, values, total):
    grouper = (jnp.arange(total, dtype=jnp.int32)[:, None] == indices[None, :]).astype(jnp.float32)
    flat = values.reshape(values.shape[0], -1)
    added = jnp.dot(
        grouper, flat, precision=lax.Precision.HIGHEST, preferred_element_type=jnp.float32
    )
    return added.reshape((total,) + values.shape[1:])


def _live_group(g, count_ref):
    return jnp.minimum(g, (count_ref[0] - 1) // GROUP)


def _forward_kernel(count_ref, row_ref, slot_ref, blk_ref, feat_ref, deg_ref, out_ref):
    g = pl.program_id(0)
    bs = blk_ref.shape[-1]
    node_count = out_ref.shape[1] - deg_ref.shape[1]
    owned = node_count // bs

    @pl.when(g == 0)
    def _():
        out_ref[:, :node_count, :] = jnp.zeros(
            (out_ref.shape[0], node_count, out_ref.shape[2]), jnp.float32
        )
        out_ref[:, node_count:, :] = deg_ref[...]

    count = count_ref[0]

    @pl.when(g * GROUP < count)
    def _():
        for j in range(GROUP):
            k = g * GROUP + j
            live = k < count
            r = row_ref[k]
            s = slot_ref[k]
            at = pl.multiple_of((r % owned) * bs, bs)
            prod = jnp.dot(blk_ref[j], feat_ref[s], preferred_element_type=jnp.float32)
            out_ref[r // owned, pl.ds(at, bs), :] += jnp.where(live, prod, 0.0)


def _backward_kernel(
    first, count_ref, row_ref, slot_ref, blk_ref, grad_ref, prev_ref, out_ref, gt_ref, acc_ref
):
    g = pl.program_id(0) + first

    @pl.when(pl.program_id(0) == 0)
    def _():
        for r in range(grad_ref.shape[0]):
            gt_ref[r] = grad_ref[r].T
        acc_ref[...] = jnp.zeros_like(acc_ref)

    count = count_ref[0]

    @pl.when(g * GROUP < count)
    def _():
        for j in range(GROUP):
            k = g * GROUP + j
            live = k < count
            r = row_ref[k]
            s = slot_ref[k]
            prod = jnp.dot(gt_ref[r], blk_ref[j], preferred_element_type=jnp.float32)
            acc_ref[s] += jnp.where(live, prod, 0.0)

    @pl.when(pl.program_id(0) == pl.num_programs(0) - 1)
    def _():
        for s in range(out_ref.shape[0]):
            out_ref[s] = acc_ref[s].T + prev_ref[s]


def aggregate_forward(counts, rows, slots, blocks, fetched, degree_rows, node_count):
    slot_total, bs, _ = blocks.shape
    fetch_total, _, width = fetched.shape
    chunks, pad, _ = degree_rows.shape
    out_rows = node_count + pad
    grid_spec = pltpu.PrefetchScalarGridSpec(
        num_scalar_prefetch=3,
        grid=(slot_total // GROUP,),
        in_specs=[
            pl.BlockSpec((GROUP, bs, bs), lambda g, c, r, s: (_live_group(g, c), 0, 0)),
            pl.BlockSpec((fetch_total, bs, width), lambda g, c, r, s: (0, 0, 0)),
            pl.BlockSpec((chunks, pad, width), lambda g, c, r, s: (0, 0, 0)),
        ],
        out_specs=pl.BlockSpec((chunks, out_rows, width), lambda g, c, r, s: (0, 0, 0)),
    )
    return pl.pallas_call(
        _forward_kernel,
        grid_spec=grid_spec,
        out_shape=jax.ShapeDtypeStruct((chunks, out_rows, width), jnp.float32),
        compiler_params=pltpu.CompilerParams(dimension_semantics=("arbitrary",)),
        cost_estimate=pl.CostEstimate(
            flops=2 * slot_total * bs * bs * width,
            bytes_accessed=blocks.size * 2 + fetched.size * 2 + chunks * out_rows * width * 4,
            transcendentals=0,
        ),
    )(counts, rows, slots, blocks, fetched, degree_rows)


def aggregate_backward(counts, rows, slots, blocks, grad_panel, previous, first, last):
    slot_total, bs, _ = blocks.shape
    panel_blocks, _, width = grad_panel.shape
    fetch_total = previous.shape[0]

    def block_at(g, c, r, s):
        return (_live_group(g + first, c), 0, 0)

    grid_spec = pltpu.PrefetchScalarGridSpec(
        num_scalar_prefetch=3,
        grid=(last - first,),
        in_specs=[
            pl.BlockSpec((GROUP, bs, bs), block_at),
            pl.BlockSpec((panel_blocks, bs, width), lambda g, c, r, s: (0, 0, 0)),
            pl.BlockSpec((fetch_total, bs, width), lambda g, c, r, s: (0, 0, 0)),
        ],
        out_specs=pl.BlockSpec((fetch_total, bs, width), lambda g, c, r, s: (0, 0, 0)),
        scratch_shapes=[
            pltpu.VMEM((panel_blocks, width, bs), jnp.bfloat16),
            pltpu.VMEM((fetch_total, width, bs), jnp.float32),
        ],
    )
    share = (last - first) * GROUP
    return pl.pallas_call(
        functools.partial(_backward_kernel, first),
        grid_spec=grid_spec,
        out_shape=jax.ShapeDtypeStruct((fetch_total, bs, width), jnp.float32),
        compiler_params=pltpu.CompilerParams(dimension_semantics=("arbitrary",)),
        cost_estimate=pl.CostEstimate(
            flops=2 * share * bs * bs * width,
            bytes_accessed=share * bs * bs * 2 + grad_panel.size * 2 + fetch_total * bs * width * 8,
            transcendentals=0,
        ),
    )(counts, rows, slots, blocks, grad_panel, previous)


def exchange_steps(axes):
    steps = []
    for name in axes:
        size = lax.axis_size(name)
        step = 1
        while step < size:
            steps.append((name, size, step))
            step *= 2
    return steps[::-1]


def spread(chunks, name):
    size = lax.axis_size(name)
    me = lax.axis_index(name)
    received = [chunks[me]]
    for offset in range(1, size):
        pairs = [(i, (i + offset) % size) for i in range(size)]
        received.append(lax.ppermute(chunks[(me + offset) % size], name, pairs))
    return jnp.stack(received)


def scatter_sum(chunks, name):
    size = lax.axis_size(name)
    me = lax.axis_index(name)
    offset = 1
    while offset < size:
        mine = (me // offset) % 2
        paired = chunks.reshape((chunks.shape[0] // 2, 2) + chunks.shape[1:])
        keep = lax.dynamic_index_in_dim(paired, mine, axis=1, keepdims=False)
        send = lax.dynamic_index_in_dim(paired, 1 - mine, axis=1, keepdims=False)
        pairs = [(i, i ^ offset) for i in range(size)]
        chunks = keep + lax.ppermute(send, name, pairs)
        offset *= 2
    return chunks[0]


def spread_sources(name):
    size = lax.axis_size(name)
    me = lax.axis_index(name)
    return (me - jnp.arange(size, dtype=jnp.int32)) % size


def exchange_add(values, step):
    name, size, offset = step
    pairs = [(i, i ^ offset) for i in range(size)]
    return values + lax.ppermute(values, name, pairs)


def on_device(
    features, w_self, w_neigh, bias, blocks, blk_row, blk_slot, counts, col_list, cotangent
):
    own_feats = features[0]
    node_count, feat_width = own_feats.shape
    block_size = blocks.shape[-1]
    owned_count = node_count // block_size
    row_count = lax.axis_size("row")
    col_count = lax.axis_size("col")
    picks_each = col_list.shape[-1]
    fetch_total = row_count * picks_each
    panel_blocks = col_count * owned_count
    wanted = col_list[0, 0]
    asked_spread = spread(wanted, "row")
    asked_for = asked_spread[spread_sources("row")]
    block_rows = blk_row[0, 0]
    block_slots = blk_slot[0, 0]
    live_count = counts[0, 0]
    own_blocks = own_feats.reshape(owned_count, block_size, feat_width)
    outgoing = select_rows(asked_for.reshape(-1), own_blocks, owned_count)
    outgoing = outgoing.reshape(row_count, picks_each, block_size, feat_width)
    arrived = spread(outgoing, "row")
    fetched = arrived.reshape(fetch_total, block_size, feat_width)
    row_me = lax.axis_index("row")
    fetch_slots = ((row_me - block_slots // picks_each) % row_count) * picks_each + (
        block_slots % picks_each
    )
    adjacency = blocks[0, 0]
    live_rows = jnp.where(
        (jnp.arange(adjacency.shape[0]) < live_count[0])[:, None],
        jnp.sum(adjacency, axis=2, dtype=jnp.float32),
        0.0,
    )
    part_deg = group_rows(block_rows, live_rows, panel_blocks)
    part_deg = part_deg.reshape(col_count, owned_count, block_size)
    part_deg = jnp.pad(part_deg, ((0, 0), (0, DEGREE_ROWS - owned_count), (0, 0)))
    packed = aggregate_forward(
        live_count, block_rows, fetch_slots, adjacency, fetched, part_deg, node_count
    )
    reduced = scatter_sum(packed, "col")
    summed = reduced[:node_count]
    degree = reduced[node_count : node_count + owned_count].reshape(node_count)
    divisor = 1.0 + degree
    neighbors = (summed / divisor[:, None]).astype(jnp.bfloat16)
    hidden = (
        jnp.dot(own_feats, w_self, preferred_element_type=jnp.float32)
        + jnp.dot(neighbors, w_neigh, preferred_element_type=jnp.float32)
        + bias
    )
    output, pullback = jax.vjp(gelu_tanh, hidden)
    grad_hidden = pullback(cotangent[0].astype(jnp.float32))[0]
    grad_round = grad_hidden.astype(jnp.bfloat16)
    local_self = jnp.einsum("nd,nh->dh", own_feats, grad_round, preferred_element_type=jnp.float32)
    local_neigh = jnp.einsum("nd,nh->dh", neighbors, grad_round, preferred_element_type=jnp.float32)
    local_bias = jnp.sum(grad_round.astype(jnp.float32), axis=0)
    hid = local_bias.shape[0]
    weight_pack = jnp.concatenate(
        [local_self, local_neigh, jnp.broadcast_to(local_bias[None], (8, hid))], axis=0
    )
    steps = exchange_steps(("col", "row"))
    cross_step = [step for step in steps if step[0] == "col"][0]
    grad_agg = (
        jnp.einsum("nh,dh->nd", grad_round, w_neigh, preferred_element_type=jnp.float32)
        / divisor[:, None]
    )
    grad_agg = grad_agg.astype(jnp.bfloat16)
    adjoint_panel = lax.all_gather(grad_agg, "col", axis=0, tiled=True)
    weight_pack = exchange_add(weight_pack, steps[0])
    weight_pack, adjoint_panel = lax.optimization_barrier((weight_pack, adjoint_panel))
    panel = adjoint_panel.reshape(panel_blocks, block_size, feat_width)
    groups = adjacency.shape[0] // GROUP
    half = groups // 2
    per_slot = jnp.zeros((fetch_total, block_size, feat_width), jnp.float32)
    per_slot = aggregate_backward(
        live_count, block_rows, block_slots, adjacency, panel, per_slot, 0, half
    )
    weight_pack = exchange_add(weight_pack, steps[1])
    weight_pack, per_slot = lax.optimization_barrier((weight_pack, per_slot))
    per_slot = aggregate_backward(
        live_count, block_rows, block_slots, adjacency, panel, per_slot, half, groups
    )
    weight_pack = exchange_add(weight_pack, steps[2])
    weight_pack, per_slot = lax.optimization_barrier((weight_pack, per_slot))
    per_slot = per_slot.reshape(row_count, picks_each, block_size, feat_width)
    returned = spread(per_slot, "row")
    weight_pack = exchange_add(weight_pack, cross_step)
    weight_pack, returned = lax.optimization_barrier((weight_pack, returned))
    incoming = group_rows(
        asked_spread.reshape(-1),
        returned.reshape(fetch_total, block_size, feat_width),
        owned_count,
    )
    incoming = incoming.reshape(node_count, feat_width)
    grad_feats = (
        jnp.einsum("nh,dh->nd", grad_round, w_self, preferred_element_type=jnp.float32) + incoming
    )
    for step in steps[3:]:
        if step != cross_step:
            weight_pack = exchange_add(weight_pack, step)
    factor = 1.0 / math.sqrt(node_count * row_count * col_count)
    grad_self = weight_pack[:feat_width] * factor
    grad_neigh = weight_pack[feat_width : 2 * feat_width] * factor
    grad_bias = weight_pack[2 * feat_width] * factor
    return (
        output.astype(jnp.bfloat16)[None],
        grad_feats.astype(jnp.bfloat16)[None],
        grad_self,
        grad_neigh,
        grad_bias,
    )


def solution(mesh):
    return jax.shard_map(
        on_device,
        mesh=mesh,
        in_specs=(
            P("col", "row", None),
            P(),
            P(),
            P(),
            P("row", "col", None, None, None),
            P("row", "col", None),
            P("row", "col", None),
            P("row", "col", None),
            P("row", "col", None, None),
            P("col", "row", None),
        ),
        out_specs=(P("col", "row", None), P("col", "row", None), P(), P(), P()),
        check_vma=False,
    )
```

```python
import functools
import math

import jax
import jax.numpy as jnp
from jax import lax
from jax.experimental import pallas as pl
from jax.experimental.pallas import tpu as pltpu
from jax.sharding import PartitionSpec as P


GROUP = 64
DEGREE_ROWS = 16


def gelu_tanh(values):
    return jax.nn.gelu(values, approximate=True)


def select_rows(indices, table, total):
    picker = (indices[:, None] == jnp.arange(total, dtype=jnp.int32)[None, :]).astype(table.dtype)
    flat = table.reshape(total, -1)
    taken = jnp.dot(picker, flat, preferred_element_type=jnp.float32).astype(table.dtype)
    return taken.reshape((indices.shape[0],) + table.shape[1:])


def group_rows(indices, values, total):
    grouper = (jnp.arange(total, dtype=jnp.int32)[:, None] == indices[None, :]).astype(jnp.float32)
    flat = values.reshape(values.shape[0], -1)
    added = jnp.dot(
        grouper, flat, precision=lax.Precision.HIGHEST, preferred_element_type=jnp.float32
    )
    return added.reshape((total,) + values.shape[1:])


def _live_group(g, count_ref):
    return jnp.minimum(g, (count_ref[0] - 1) // GROUP)


def _forward_kernel(count_ref, row_ref, slot_ref, blk_ref, feat_ref, deg_ref, out_ref):
    g = pl.program_id(0)
    bs = blk_ref.shape[-1]
    node_count = out_ref.shape[1] - deg_ref.shape[1]
    owned = node_count // bs

    @pl.when(g == 0)
    def _():
        out_ref[:, :node_count, :] = jnp.zeros(
            (out_ref.shape[0], node_count, out_ref.shape[2]), jnp.float32
        )
        out_ref[:, node_count:, :] = deg_ref[...]

    count = count_ref[0]

    @pl.when(g * GROUP < count)
    def _():
        for j in range(GROUP):
            k = g * GROUP + j
            live = k < count
            r = row_ref[k]
            s = slot_ref[k]
            at = pl.multiple_of((r % owned) * bs, bs)
            prod = jnp.dot(blk_ref[j], feat_ref[s], preferred_element_type=jnp.float32)
            out_ref[r // owned, pl.ds(at, bs), :] += jnp.where(live, prod, 0.0)


def _backward_kernel(first, count_ref, row_ref, slot_ref, blk_ref, grad_ref, *refs):
    if len(refs) == 4:
        prev_ref, out_ref, gt_ref, acc_ref = refs
    else:
        prev_ref = None
        out_ref, gt_ref, acc_ref = refs
    g = pl.program_id(0) + first

    @pl.when(pl.program_id(0) == 0)
    def _():
        for r in range(grad_ref.shape[0]):
            gt_ref[r] = grad_ref[r].T
        acc_ref[...] = jnp.zeros_like(acc_ref)

    count = count_ref[0]

    @pl.when(g * GROUP < count)
    def _():
        for j in range(GROUP):
            k = g * GROUP + j
            live = k < count
            r = row_ref[k]
            s = slot_ref[k]
            prod = jnp.dot(gt_ref[r], blk_ref[j], preferred_element_type=jnp.float32)
            acc_ref[s] += jnp.where(live, prod, 0.0)

    @pl.when(pl.program_id(0) == pl.num_programs(0) - 1)
    def _():
        for s in range(out_ref.shape[0]):
            if prev_ref is None:
                out_ref[s] = acc_ref[s].T
            else:
                out_ref[s] = acc_ref[s].T + prev_ref[s]


def aggregate_forward(counts, rows, slots, blocks, fetched, degree_rows, node_count):
    slot_total, bs, _ = blocks.shape
    fetch_total, _, width = fetched.shape
    chunks, pad, _ = degree_rows.shape
    out_rows = node_count + pad
    grid_spec = pltpu.PrefetchScalarGridSpec(
        num_scalar_prefetch=3,
        grid=(slot_total // GROUP,),
        in_specs=[
            pl.BlockSpec((GROUP, bs, bs), lambda g, c, r, s: (_live_group(g, c), 0, 0)),
            pl.BlockSpec((fetch_total, bs, width), lambda g, c, r, s: (0, 0, 0)),
            pl.BlockSpec((chunks, pad, width), lambda g, c, r, s: (0, 0, 0)),
        ],
        out_specs=pl.BlockSpec((chunks, out_rows, width), lambda g, c, r, s: (0, 0, 0)),
    )
    return pl.pallas_call(
        _forward_kernel,
        grid_spec=grid_spec,
        out_shape=jax.ShapeDtypeStruct((chunks, out_rows, width), jnp.float32),
        compiler_params=pltpu.CompilerParams(dimension_semantics=("arbitrary",)),
        cost_estimate=pl.CostEstimate(
            flops=2 * slot_total * bs * bs * width,
            bytes_accessed=blocks.size * 2 + fetched.size * 2 + chunks * out_rows * width * 4,
            transcendentals=0,
        ),
    )(counts, rows, slots, blocks, fetched, degree_rows)


def aggregate_backward(counts, rows, slots, blocks, grad_panel, previous, fetch_total, first, last):
    slot_total, bs, _ = blocks.shape
    panel_blocks, _, width = grad_panel.shape
    extra = [] if previous is None else [previous]

    def block_at(g, c, r, s):
        return (_live_group(g + first, c), 0, 0)

    grid_spec = pltpu.PrefetchScalarGridSpec(
        num_scalar_prefetch=3,
        grid=(last - first,),
        in_specs=[
            pl.BlockSpec((GROUP, bs, bs), block_at),
            pl.BlockSpec((panel_blocks, bs, width), lambda g, c, r, s: (0, 0, 0)),
        ]
        + [pl.BlockSpec((fetch_total, bs, width), lambda g, c, r, s: (0, 0, 0))] * len(extra),
        out_specs=pl.BlockSpec((fetch_total, bs, width), lambda g, c, r, s: (0, 0, 0)),
        scratch_shapes=[
            pltpu.VMEM((panel_blocks, width, bs), jnp.bfloat16),
            pltpu.VMEM((fetch_total, width, bs), jnp.float32),
        ],
    )
    share = (last - first) * GROUP
    return pl.pallas_call(
        functools.partial(_backward_kernel, first),
        grid_spec=grid_spec,
        out_shape=jax.ShapeDtypeStruct((fetch_total, bs, width), jnp.float32),
        compiler_params=pltpu.CompilerParams(dimension_semantics=("arbitrary",)),
        cost_estimate=pl.CostEstimate(
            flops=2 * share * bs * bs * width,
            bytes_accessed=share * bs * bs * 2 + grad_panel.size * 2 + fetch_total * bs * width * 8,
            transcendentals=0,
        ),
    )(counts, rows, slots, blocks, grad_panel, *extra)


def exchange_steps(axes):
    steps = []
    for name in axes:
        size = lax.axis_size(name)
        step = 1
        while step < size:
            steps.append((name, size, step))
            step *= 2
    return steps[::-1]


def spread(chunks, name):
    size = lax.axis_size(name)
    me = lax.axis_index(name)
    received = [chunks[me]]
    for offset in range(1, size):
        pairs = [(i, (i + offset) % size) for i in range(size)]
        received.append(lax.ppermute(chunks[(me + offset) % size], name, pairs))
    return jnp.stack(received)


def scatter_sum(chunks, name):
    size = lax.axis_size(name)
    me = lax.axis_index(name)
    offset = 1
    while offset < size:
        mine = (me // offset) % 2
        paired = chunks.reshape((chunks.shape[0] // 2, 2) + chunks.shape[1:])
        keep = lax.dynamic_index_in_dim(paired, mine, axis=1, keepdims=False)
        send = lax.dynamic_index_in_dim(paired, 1 - mine, axis=1, keepdims=False)
        pairs = [(i, i ^ offset) for i in range(size)]
        chunks = keep + lax.ppermute(send, name, pairs)
        offset *= 2
    return chunks[0]


def spread_sources(name):
    size = lax.axis_size(name)
    me = lax.axis_index(name)
    return (me - jnp.arange(size, dtype=jnp.int32)) % size


def exchange_add(values, step):
    name, size, offset = step
    pairs = [(i, i ^ offset) for i in range(size)]
    return values + lax.ppermute(values, name, pairs)


def on_device(
    features, w_self, w_neigh, bias, blocks, blk_row, blk_slot, counts, col_list, cotangent
):
    own_feats = features[0]
    node_count, feat_width = own_feats.shape
    block_size = blocks.shape[-1]
    owned_count = node_count // block_size
    row_count = lax.axis_size("row")
    col_count = lax.axis_size("col")
    picks_each = col_list.shape[-1]
    fetch_total = row_count * picks_each
    panel_blocks = col_count * owned_count
    wanted = col_list[0, 0]
    asked_for = lax.all_to_all(wanted, "row", split_axis=0, concat_axis=0, tiled=True)
    block_rows = blk_row[0, 0]
    block_slots = blk_slot[0, 0]
    live_count = counts[0, 0]
    own_blocks = own_feats.reshape(owned_count, block_size, feat_width)
    outgoing = select_rows(asked_for.reshape(-1), own_blocks, owned_count)
    outgoing = outgoing.reshape(row_count, picks_each, block_size, feat_width)
    arrived = lax.all_to_all(outgoing, "row", split_axis=0, concat_axis=0, tiled=True)
    fetched = arrived.reshape(fetch_total, block_size, feat_width)
    adjacency = blocks[0, 0]
    live_rows = jnp.where(
        (jnp.arange(adjacency.shape[0]) < live_count[0])[:, None],
        jnp.sum(adjacency, axis=2, dtype=jnp.float32),
        0.0,
    )
    part_deg = group_rows(block_rows, live_rows, panel_blocks)
    part_deg = part_deg.reshape(col_count, owned_count, block_size)
    part_deg = jnp.pad(part_deg, ((0, 0), (0, DEGREE_ROWS - owned_count), (0, 0)))
    packed = aggregate_forward(
        live_count, block_rows, block_slots, adjacency, fetched, part_deg, node_count
    )
    reduced = scatter_sum(packed, "col")
    summed = reduced[:node_count]
    degree = reduced[node_count : node_count + owned_count].reshape(node_count)
    divisor = 1.0 + degree
    neighbors = (summed / divisor[:, None]).astype(jnp.bfloat16)
    hidden = (
        jnp.dot(own_feats, w_self, preferred_element_type=jnp.float32)
        + jnp.dot(neighbors, w_neigh, preferred_element_type=jnp.float32)
        + bias
    )
    output, pullback = jax.vjp(gelu_tanh, hidden)
    grad_hidden = pullback(cotangent[0].astype(jnp.float32))[0]
    grad_round = grad_hidden.astype(jnp.bfloat16)
    local_self = jnp.einsum("nd,nh->dh", own_feats, grad_round, preferred_element_type=jnp.float32)
    local_neigh = jnp.einsum("nd,nh->dh", neighbors, grad_round, preferred_element_type=jnp.float32)
    local_bias = jnp.sum(grad_round.astype(jnp.float32), axis=0)
    hid = local_bias.shape[0]
    weight_pack = jnp.concatenate(
        [local_self, local_neigh, jnp.broadcast_to(local_bias[None], (8, hid))], axis=0
    )
    steps = exchange_steps(("col", "row"))
    cross_step = [step for step in steps if step[0] == "col"][0]
    grad_agg = (
        jnp.einsum("nh,dh->nd", grad_round, w_neigh, preferred_element_type=jnp.float32)
        / divisor[:, None]
    )
    grad_agg = grad_agg.astype(jnp.bfloat16)
    adjoint_panel = lax.all_gather(grad_agg, "col", axis=0, tiled=True)
    weight_pack = exchange_add(weight_pack, steps[0])
    weight_pack, adjoint_panel = lax.optimization_barrier((weight_pack, adjoint_panel))
    panel = adjoint_panel.reshape(panel_blocks, block_size, feat_width)
    groups = adjacency.shape[0] // GROUP
    half = groups // 2
    per_slot = aggregate_backward(
        live_count, block_rows, block_slots, adjacency, panel, None, fetch_total, 0, half
    )
    weight_pack = exchange_add(weight_pack, steps[1])
    weight_pack, per_slot = lax.optimization_barrier((weight_pack, per_slot))
    per_slot = aggregate_backward(
        live_count, block_rows, block_slots, adjacency, panel, per_slot, fetch_total, half, groups
    )
    weight_pack = exchange_add(weight_pack, steps[2])
    weight_pack, per_slot = lax.optimization_barrier((weight_pack, per_slot))
    per_slot = per_slot.reshape(row_count, picks_each, block_size, feat_width)
    returned = spread(per_slot, "row")
    weight_pack = exchange_add(weight_pack, cross_step)
    weight_pack, returned = lax.optimization_barrier((weight_pack, returned))
    incoming = group_rows(
        asked_for[spread_sources("row")].reshape(-1),
        returned.reshape(fetch_total, block_size, feat_width),
        owned_count,
    )
    incoming = incoming.reshape(node_count, feat_width)
    grad_feats = (
        jnp.einsum("nh,dh->nd", grad_round, w_self, preferred_element_type=jnp.float32) + incoming
    )
    for step in steps[3:]:
        if step != cross_step:
            weight_pack = exchange_add(weight_pack, step)
    factor = 1.0 / math.sqrt(node_count * row_count * col_count)
    grad_self = weight_pack[:feat_width] * factor
    grad_neigh = weight_pack[feat_width : 2 * feat_width] * factor
    grad_bias = weight_pack[2 * feat_width] * factor
    return (
        output.astype(jnp.bfloat16)[None],
        grad_feats.astype(jnp.bfloat16)[None],
        grad_self,
        grad_neigh,
        grad_bias,
    )


def solution(mesh):
    return jax.shard_map(
        on_device,
        mesh=mesh,
        in_specs=(
            P("col", "row", None),
            P(),
            P(),
            P(),
            P("row", "col", None, None, None),
            P("row", "col", None),
            P("row", "col", None),
            P("row", "col", None),
            P("row", "col", None, None),
            P("col", "row", None),
        ),
        out_specs=(P("col", "row", None), P("col", "row", None), P(), P(), P()),
        check_vma=False,
    )
```

```python
import functools
import math

import jax
import jax.numpy as jnp
from jax import lax
from jax.experimental import pallas as pl
from jax.experimental.pallas import tpu as pltpu
from jax.sharding import PartitionSpec as P


FORWARD_GROUP = 160
BACKWARD_GROUP = 80
DEGREE_ROWS = 16


def gelu_tanh(values):
    return jax.nn.gelu(values, approximate=True)


def select_rows(indices, table, total):
    picker = (indices[:, None] == jnp.arange(total, dtype=jnp.int32)[None, :]).astype(table.dtype)
    flat = table.reshape(total, -1)
    taken = jnp.dot(picker, flat, preferred_element_type=jnp.float32).astype(table.dtype)
    return taken.reshape((indices.shape[0],) + table.shape[1:])


def group_rows(indices, values, total):
    grouper = (jnp.arange(total, dtype=jnp.int32)[:, None] == indices[None, :]).astype(jnp.float32)
    flat = values.reshape(values.shape[0], -1)
    added = jnp.dot(
        grouper, flat, precision=lax.Precision.HIGHEST, preferred_element_type=jnp.float32
    )
    return added.reshape((total,) + values.shape[1:])


def _live_group(g, count_ref, group):
    return jnp.minimum(g, (count_ref[0] - 1) // group)


def _forward_kernel(count_ref, row_ref, slot_ref, blk_ref, feat_ref, deg_ref, out_ref):
    g = pl.program_id(0)
    bs = blk_ref.shape[-1]
    node_count = out_ref.shape[1] - deg_ref.shape[1]
    owned = node_count // bs

    @pl.when(g == 0)
    def _():
        out_ref[:, :node_count, :] = jnp.zeros(
            (out_ref.shape[0], node_count, out_ref.shape[2]), jnp.float32
        )
        out_ref[:, node_count:, :] = deg_ref[...]

    count = count_ref[0]

    @pl.when(g * FORWARD_GROUP < count)
    def _():
        for j in range(FORWARD_GROUP):
            k = g * FORWARD_GROUP + j
            live = k < count
            r = row_ref[k]
            s = slot_ref[k]
            at = pl.multiple_of((r % owned) * bs, bs)
            prod = jnp.dot(blk_ref[j], feat_ref[s], preferred_element_type=jnp.float32)
            out_ref[r // owned, pl.ds(at, bs), :] += jnp.where(live, prod, 0.0)


def _backward_kernel(first, count_ref, row_ref, slot_ref, blk_ref, grad_ref, *refs):
    if len(refs) == 4:
        prev_ref, out_ref, gt_ref, acc_ref = refs
    else:
        prev_ref = None
        out_ref, gt_ref, acc_ref = refs
    g = pl.program_id(0) + first

    @pl.when(pl.program_id(0) == 0)
    def _():
        for r in range(grad_ref.shape[0]):
            gt_ref[r] = grad_ref[r].T
        acc_ref[...] = jnp.zeros_like(acc_ref)

    count = count_ref[0]

    @pl.when(g * BACKWARD_GROUP < count)
    def _():
        for j in range(BACKWARD_GROUP):
            k = g * BACKWARD_GROUP + j
            live = k < count
            r = row_ref[k]
            s = slot_ref[k]
            prod = jnp.dot(gt_ref[r], blk_ref[j], preferred_element_type=jnp.float32)
            acc_ref[s] += jnp.where(live, prod, 0.0)

    @pl.when(pl.program_id(0) == pl.num_programs(0) - 1)
    def _():
        for s in range(out_ref.shape[0]):
            if prev_ref is None:
                out_ref[s] = acc_ref[s].T
            else:
                out_ref[s] = acc_ref[s].T + prev_ref[s]


def aggregate_forward(counts, rows, slots, blocks, fetched, degree_rows, node_count):
    slot_total, bs, _ = blocks.shape
    fetch_total, _, width = fetched.shape
    chunks, pad, _ = degree_rows.shape
    out_rows = node_count + pad

    def block_at(g, c, r, s):
        return (_live_group(g, c, FORWARD_GROUP), 0, 0)

    grid_spec = pltpu.PrefetchScalarGridSpec(
        num_scalar_prefetch=3,
        grid=(slot_total // FORWARD_GROUP,),
        in_specs=[
            pl.BlockSpec((FORWARD_GROUP, bs, bs), block_at),
            pl.BlockSpec((fetch_total, bs, width), lambda g, c, r, s: (0, 0, 0)),
            pl.BlockSpec((chunks, pad, width), lambda g, c, r, s: (0, 0, 0)),
        ],
        out_specs=pl.BlockSpec((chunks, out_rows, width), lambda g, c, r, s: (0, 0, 0)),
    )
    return pl.pallas_call(
        _forward_kernel,
        grid_spec=grid_spec,
        out_shape=jax.ShapeDtypeStruct((chunks, out_rows, width), jnp.float32),
        compiler_params=pltpu.CompilerParams(dimension_semantics=("arbitrary",)),
        cost_estimate=pl.CostEstimate(
            flops=2 * slot_total * bs * bs * width,
            bytes_accessed=blocks.size * 2 + fetched.size * 2 + chunks * out_rows * width * 4,
            transcendentals=0,
        ),
    )(counts, rows, slots, blocks, fetched, degree_rows)


def aggregate_backward(counts, rows, slots, blocks, grad_panel, previous, fetch_total, first, last):
    slot_total, bs, _ = blocks.shape
    panel_blocks, _, width = grad_panel.shape
    extra = [] if previous is None else [previous]

    def block_at(g, c, r, s):
        return (_live_group(g + first, c, BACKWARD_GROUP), 0, 0)

    grid_spec = pltpu.PrefetchScalarGridSpec(
        num_scalar_prefetch=3,
        grid=(last - first,),
        in_specs=[
            pl.BlockSpec((BACKWARD_GROUP, bs, bs), block_at),
            pl.BlockSpec((panel_blocks, bs, width), lambda g, c, r, s: (0, 0, 0)),
        ]
        + [pl.BlockSpec((fetch_total, bs, width), lambda g, c, r, s: (0, 0, 0))] * len(extra),
        out_specs=pl.BlockSpec((fetch_total, bs, width), lambda g, c, r, s: (0, 0, 0)),
        scratch_shapes=[
            pltpu.VMEM((panel_blocks, width, bs), jnp.bfloat16),
            pltpu.VMEM((fetch_total, width, bs), jnp.float32),
        ],
    )
    share = (last - first) * BACKWARD_GROUP
    return pl.pallas_call(
        functools.partial(_backward_kernel, first),
        grid_spec=grid_spec,
        out_shape=jax.ShapeDtypeStruct((fetch_total, bs, width), jnp.float32),
        compiler_params=pltpu.CompilerParams(dimension_semantics=("arbitrary",)),
        cost_estimate=pl.CostEstimate(
            flops=2 * share * bs * bs * width,
            bytes_accessed=share * bs * bs * 2 + grad_panel.size * 2 + fetch_total * bs * width * 8,
            transcendentals=0,
        ),
    )(counts, rows, slots, blocks, grad_panel, *extra)


def exchange_steps(axes):
    steps = []
    for name in axes:
        size = lax.axis_size(name)
        step = 1
        while step < size:
            steps.append((name, size, step))
            step *= 2
    return steps[::-1]


def spread(chunks, name):
    size = lax.axis_size(name)
    me = lax.axis_index(name)
    received = [chunks[me]]
    for offset in range(1, size):
        pairs = [(i, (i + offset) % size) for i in range(size)]
        received.append(lax.ppermute(chunks[(me + offset) % size], name, pairs))
    return jnp.stack(received)


def scatter_sum(chunks, name):
    size = lax.axis_size(name)
    me = lax.axis_index(name)
    offset = 1
    while offset < size:
        mine = (me // offset) % 2
        paired = chunks.reshape((chunks.shape[0] // 2, 2) + chunks.shape[1:])
        keep = lax.dynamic_index_in_dim(paired, mine, axis=1, keepdims=False)
        send = lax.dynamic_index_in_dim(paired, 1 - mine, axis=1, keepdims=False)
        pairs = [(i, i ^ offset) for i in range(size)]
        chunks = keep + lax.ppermute(send, name, pairs)
        offset *= 2
    return chunks[0]


def spread_sources(name):
    size = lax.axis_size(name)
    me = lax.axis_index(name)
    return (me - jnp.arange(size, dtype=jnp.int32)) % size


def exchange_add(values, step):
    name, size, offset = step
    pairs = [(i, i ^ offset) for i in range(size)]
    return values + lax.ppermute(values, name, pairs)


def on_device(
    features, w_self, w_neigh, bias, blocks, blk_row, blk_slot, counts, col_list, cotangent
):
    own_feats = features[0]
    node_count, feat_width = own_feats.shape
    block_size = blocks.shape[-1]
    owned_count = node_count // block_size
    row_count = lax.axis_size("row")
    col_count = lax.axis_size("col")
    picks_each = col_list.shape[-1]
    fetch_total = row_count * picks_each
    panel_blocks = col_count * owned_count
    wanted = col_list[0, 0]
    asked_for = lax.all_to_all(wanted, "row", split_axis=0, concat_axis=0, tiled=True)
    block_rows = blk_row[0, 0]
    block_slots = blk_slot[0, 0]
    live_count = counts[0, 0]
    own_blocks = own_feats.reshape(owned_count, block_size, feat_width)
    outgoing = select_rows(asked_for.reshape(-1), own_blocks, owned_count)
    outgoing = outgoing.reshape(row_count, picks_each, block_size, feat_width)
    arrived = lax.all_to_all(outgoing, "row", split_axis=0, concat_axis=0, tiled=True)
    fetched = arrived.reshape(fetch_total, block_size, feat_width)
    adjacency = blocks[0, 0]
    live_rows = jnp.where(
        (jnp.arange(adjacency.shape[0]) < live_count[0])[:, None],
        jnp.sum(adjacency, axis=2, dtype=jnp.float32),
        0.0,
    )
    part_deg = group_rows(block_rows, live_rows, panel_blocks)
    part_deg = part_deg.reshape(col_count, owned_count, block_size)
    part_deg = jnp.pad(part_deg, ((0, 0), (0, DEGREE_ROWS - owned_count), (0, 0)))
    packed = aggregate_forward(
        live_count, block_rows, block_slots, adjacency, fetched, part_deg, node_count
    )
    reduced = scatter_sum(packed, "col")
    summed = reduced[:node_count]
    degree = reduced[node_count : node_count + owned_count].reshape(node_count)
    divisor = 1.0 + degree
    neighbors = (summed / divisor[:, None]).astype(jnp.bfloat16)
    hidden = (
        jnp.dot(own_feats, w_self, preferred_element_type=jnp.float32)
        + jnp.dot(neighbors, w_neigh, preferred_element_type=jnp.float32)
        + bias
    )
    output, pullback = jax.vjp(gelu_tanh, hidden)
    grad_hidden = pullback(cotangent[0].astype(jnp.float32))[0]
    grad_round = grad_hidden.astype(jnp.bfloat16)
    local_self = jnp.einsum("nd,nh->dh", own_feats, grad_round, preferred_element_type=jnp.float32)
    local_neigh = jnp.einsum("nd,nh->dh", neighbors, grad_round, preferred_element_type=jnp.float32)
    local_bias = jnp.sum(grad_round.astype(jnp.float32), axis=0)
    hid = local_bias.shape[0]
    weight_pack = jnp.concatenate(
        [local_self, local_neigh, jnp.broadcast_to(local_bias[None], (8, hid))], axis=0
    )
    steps = exchange_steps(("col", "row"))
    cross_step = [step for step in steps if step[0] == "col"][0]
    grad_agg = (
        jnp.einsum("nh,dh->nd", grad_round, w_neigh, preferred_element_type=jnp.float32)
        / divisor[:, None]
    )
    grad_agg = grad_agg.astype(jnp.bfloat16)
    adjoint_panel = lax.all_gather(grad_agg, "col", axis=0, tiled=True)
    weight_pack = exchange_add(weight_pack, steps[0])
    weight_pack, adjoint_panel = lax.optimization_barrier((weight_pack, adjoint_panel))
    panel = adjoint_panel.reshape(panel_blocks, block_size, feat_width)
    groups = adjacency.shape[0] // BACKWARD_GROUP
    half = groups // 2
    per_slot = aggregate_backward(
        live_count, block_rows, block_slots, adjacency, panel, None, fetch_total, 0, half
    )
    weight_pack = exchange_add(weight_pack, steps[1])
    weight_pack, per_slot = lax.optimization_barrier((weight_pack, per_slot))
    per_slot = aggregate_backward(
        live_count, block_rows, block_slots, adjacency, panel, per_slot, fetch_total, half, groups
    )
    weight_pack = exchange_add(weight_pack, steps[2])
    weight_pack, per_slot = lax.optimization_barrier((weight_pack, per_slot))
    per_slot = per_slot.reshape(row_count, picks_each, block_size, feat_width)
    returned = spread(per_slot, "row")
    weight_pack = exchange_add(weight_pack, cross_step)
    weight_pack, returned = lax.optimization_barrier((weight_pack, returned))
    incoming = group_rows(
        asked_for[spread_sources("row")].reshape(-1),
        returned.reshape(fetch_total, block_size, feat_width),
        owned_count,
    )
    incoming = incoming.reshape(node_count, feat_width)
    grad_feats = (
        jnp.einsum("nh,dh->nd", grad_round, w_self, preferred_element_type=jnp.float32) + incoming
    )
    for step in steps[3:]:
        if step != cross_step:
            weight_pack = exchange_add(weight_pack, step)
    factor = 1.0 / math.sqrt(node_count * row_count * col_count)
    grad_self = weight_pack[:feat_width] * factor
    grad_neigh = weight_pack[feat_width : 2 * feat_width] * factor
    grad_bias = weight_pack[2 * feat_width] * factor
    return (
        output.astype(jnp.bfloat16)[None],
        grad_feats.astype(jnp.bfloat16)[None],
        grad_self,
        grad_neigh,
        grad_bias,
    )


def solution(mesh):
    return jax.shard_map(
        on_device,
        mesh=mesh,
        in_specs=(
            P("col", "row", None),
            P(),
            P(),
            P(),
            P("row", "col", None, None, None),
            P("row", "col", None),
            P("row", "col", None),
            P("row", "col", None),
            P("row", "col", None, None),
            P("col", "row", None),
        ),
        out_specs=(P("col", "row", None), P("col", "row", None), P(), P(), P()),
        check_vma=False,
    )
```

```python
import functools
import math

import jax
import jax.numpy as jnp
from jax import lax
from jax.experimental import pallas as pl
from jax.experimental.pallas import tpu as pltpu
from jax.sharding import PartitionSpec as P


FORWARD_GROUP = 160
BACKWARD_GROUP = 80
DEGREE_ROWS = 16


def gelu_tanh(values):
    return jax.nn.gelu(values, approximate=True)


def select_rows(indices, table, total):
    picker = (indices[:, None] == jnp.arange(total, dtype=jnp.int32)[None, :]).astype(table.dtype)
    flat = table.reshape(total, -1)
    taken = jnp.dot(picker, flat, preferred_element_type=jnp.float32).astype(table.dtype)
    return taken.reshape((indices.shape[0],) + table.shape[1:])


def group_rows(indices, values, total):
    grouper = (jnp.arange(total, dtype=jnp.int32)[:, None] == indices[None, :]).astype(jnp.float32)
    flat = values.reshape(values.shape[0], -1)
    added = jnp.dot(
        grouper, flat, precision=lax.Precision.HIGHEST, preferred_element_type=jnp.float32
    )
    return added.reshape((total,) + values.shape[1:])


def _live_group(g, count_ref, group):
    return jnp.minimum(g, (count_ref[0] - 1) // group)


def _forward_kernel(count_ref, row_ref, slot_ref, blk_ref, feat_ref, deg_ref, out_ref):
    g = pl.program_id(0)
    bs = blk_ref.shape[-1]
    node_count = out_ref.shape[1] - deg_ref.shape[1]
    owned = node_count // bs

    @pl.when(g == 0)
    def _():
        out_ref[:, :node_count, :] = jnp.zeros(
            (out_ref.shape[0], node_count, out_ref.shape[2]), jnp.float32
        )
        out_ref[:, node_count:, :] = deg_ref[...]

    count = count_ref[0]

    @pl.when(g * FORWARD_GROUP < count)
    def _():
        for j in range(FORWARD_GROUP):
            k = g * FORWARD_GROUP + j
            live = k < count
            r = row_ref[k]
            s = slot_ref[k]
            at = pl.multiple_of((r % owned) * bs, bs)
            prod = jnp.dot(blk_ref[j], feat_ref[s], preferred_element_type=jnp.float32)
            out_ref[r // owned, pl.ds(at, bs), :] += jnp.where(live, prod, 0.0)


def _backward_kernel(first, final, count_ref, row_ref, slot_ref, blk_ref, grad_ref, *refs):
    if first == 0:
        out_ref, gt_out_ref, acc_ref = refs
        gt_ref = gt_out_ref
    else:
        prev_ref, out_ref, acc_ref = refs
        gt_ref = grad_ref
    g = pl.program_id(0) + first

    @pl.when(pl.program_id(0) == 0)
    def _():
        if first == 0:
            for r in range(grad_ref.shape[0]):
                gt_ref[r] = grad_ref[r].T
            acc_ref[...] = jnp.zeros_like(acc_ref)
        else:
            acc_ref[...] = prev_ref[...]

    count = count_ref[0]

    @pl.when(g * BACKWARD_GROUP < count)
    def _():
        for j in range(BACKWARD_GROUP):
            k = g * BACKWARD_GROUP + j
            live = k < count
            r = row_ref[k]
            s = slot_ref[k]
            prod = jnp.dot(gt_ref[r], blk_ref[j], preferred_element_type=jnp.float32)
            acc_ref[s] += jnp.where(live, prod, 0.0)

    @pl.when(pl.program_id(0) == pl.num_programs(0) - 1)
    def _():
        for s in range(out_ref.shape[0]):
            out_ref[s] = acc_ref[s].T if final else acc_ref[s]


def aggregate_forward(counts, rows, slots, blocks, fetched, degree_rows, node_count):
    slot_total, bs, _ = blocks.shape
    fetch_total, _, width = fetched.shape
    chunks, pad, _ = degree_rows.shape
    out_rows = node_count + pad

    def block_at(g, c, r, s):
        return (_live_group(g, c, FORWARD_GROUP), 0, 0)

    grid_spec = pltpu.PrefetchScalarGridSpec(
        num_scalar_prefetch=3,
        grid=(slot_total // FORWARD_GROUP,),
        in_specs=[
            pl.BlockSpec((FORWARD_GROUP, bs, bs), block_at),
            pl.BlockSpec((fetch_total, bs, width), lambda g, c, r, s: (0, 0, 0)),
            pl.BlockSpec((chunks, pad, width), lambda g, c, r, s: (0, 0, 0)),
        ],
        out_specs=pl.BlockSpec((chunks, out_rows, width), lambda g, c, r, s: (0, 0, 0)),
    )
    return pl.pallas_call(
        _forward_kernel,
        grid_spec=grid_spec,
        out_shape=jax.ShapeDtypeStruct((chunks, out_rows, width), jnp.float32),
        compiler_params=pltpu.CompilerParams(dimension_semantics=("arbitrary",)),
        cost_estimate=pl.CostEstimate(
            flops=2 * slot_total * bs * bs * width,
            bytes_accessed=blocks.size * 2 + fetched.size * 2 + chunks * out_rows * width * 4,
            transcendentals=0,
        ),
    )(counts, rows, slots, blocks, fetched, degree_rows)


def aggregate_backward(
    counts, rows, slots, blocks, grad_panel, previous, fetch_total, first, last, final
):
    slot_total, bs, _ = blocks.shape
    panel_blocks, _, width = grad_panel.shape

    def block_at(g, c, r, s):
        return (_live_group(g + first, c, BACKWARD_GROUP), 0, 0)

    whole = lambda g, c, r, s: (0, 0, 0)
    in_specs = [pl.BlockSpec((BACKWARD_GROUP, bs, bs), block_at), pl.BlockSpec(grad_panel.shape, whole)]
    out_shape = [jax.ShapeDtypeStruct((fetch_total, bs, width), jnp.float32)]
    extra = []
    if previous is None:
        out_shape.append(jax.ShapeDtypeStruct((panel_blocks, width, bs), jnp.bfloat16))
    else:
        in_specs.append(pl.BlockSpec(previous.shape, whole))
        extra.append(previous)
    grid_spec = pltpu.PrefetchScalarGridSpec(
        num_scalar_prefetch=3,
        grid=(last - first,),
        in_specs=in_specs,
        out_specs=[pl.BlockSpec(o.shape, whole) for o in out_shape],
        scratch_shapes=[pltpu.VMEM((fetch_total, width, bs), jnp.float32)],
    )
    share = (last - first) * BACKWARD_GROUP
    result = pl.pallas_call(
        functools.partial(_backward_kernel, first, final),
        grid_spec=grid_spec,
        out_shape=out_shape,
        compiler_params=pltpu.CompilerParams(dimension_semantics=("arbitrary",)),
        cost_estimate=pl.CostEstimate(
            flops=2 * share * bs * bs * width,
            bytes_accessed=share * bs * bs * 2 + grad_panel.size * 4 + fetch_total * bs * width * 8,
            transcendentals=0,
        ),
    )(counts, rows, slots, blocks, grad_panel, *extra)
    return result if previous is None else result[0]


def exchange_steps(axes):
    steps = []
    for name in axes:
        size = lax.axis_size(name)
        step = 1
        while step < size:
            steps.append((name, size, step))
            step *= 2
    return steps[::-1]


def spread(chunks, name):
    size = lax.axis_size(name)
    me = lax.axis_index(name)
    received = [chunks[me]]
    for offset in range(1, size):
        pairs = [(i, (i + offset) % size) for i in range(size)]
        received.append(lax.ppermute(chunks[(me + offset) % size], name, pairs))
    return jnp.stack(received)


def scatter_sum(chunks, name):
    size = lax.axis_size(name)
    me = lax.axis_index(name)
    offset = 1
    while offset < size:
        mine = (me // offset) % 2
        paired = chunks.reshape((chunks.shape[0] // 2, 2) + chunks.shape[1:])
        keep = lax.dynamic_index_in_dim(paired, mine, axis=1, keepdims=False)
        send = lax.dynamic_index_in_dim(paired, 1 - mine, axis=1, keepdims=False)
        pairs = [(i, i ^ offset) for i in range(size)]
        chunks = keep + lax.ppermute(send, name, pairs)
        offset *= 2
    return chunks[0]


def spread_sources(name):
    size = lax.axis_size(name)
    me = lax.axis_index(name)
    return (me - jnp.arange(size, dtype=jnp.int32)) % size


def exchange_add(values, step):
    name, size, offset = step
    pairs = [(i, i ^ offset) for i in range(size)]
    return values + lax.ppermute(values, name, pairs)


def on_device(
    features, w_self, w_neigh, bias, blocks, blk_row, blk_slot, counts, col_list, cotangent
):
    own_feats = features[0]
    node_count, feat_width = own_feats.shape
    block_size = blocks.shape[-1]
    owned_count = node_count // block_size
    row_count = lax.axis_size("row")
    col_count = lax.axis_size("col")
    picks_each = col_list.shape[-1]
    fetch_total = row_count * picks_each
    panel_blocks = col_count * owned_count
    wanted = col_list[0, 0]
    asked_for = lax.all_to_all(wanted, "row", split_axis=0, concat_axis=0, tiled=True)
    block_rows = blk_row[0, 0]
    block_slots = blk_slot[0, 0]
    live_count = counts[0, 0]
    own_blocks = own_feats.reshape(owned_count, block_size, feat_width)
    outgoing = select_rows(asked_for.reshape(-1), own_blocks, owned_count)
    outgoing = outgoing.reshape(row_count, picks_each, block_size, feat_width)
    arrived = lax.all_to_all(outgoing, "row", split_axis=0, concat_axis=0, tiled=True)
    fetched = arrived.reshape(fetch_total, block_size, feat_width)
    adjacency = blocks[0, 0]
    live_rows = jnp.where(
        (jnp.arange(adjacency.shape[0]) < live_count[0])[:, None],
        jnp.sum(adjacency, axis=2, dtype=jnp.float32),
        0.0,
    )
    part_deg = group_rows(block_rows, live_rows, panel_blocks)
    part_deg = part_deg.reshape(col_count, owned_count, block_size)
    part_deg = jnp.pad(part_deg, ((0, 0), (0, DEGREE_ROWS - owned_count), (0, 0)))
    packed = aggregate_forward(
        live_count, block_rows, block_slots, adjacency, fetched, part_deg, node_count
    )
    reduced = scatter_sum(packed, "col")
    summed = reduced[:node_count]
    degree = reduced[node_count : node_count + owned_count].reshape(node_count)
    divisor = 1.0 + degree
    neighbors = (summed / divisor[:, None]).astype(jnp.bfloat16)
    hidden = (
        jnp.dot(own_feats, w_self, preferred_element_type=jnp.float32)
        + jnp.dot(neighbors, w_neigh, preferred_element_type=jnp.float32)
        + bias
    )
    output, pullback = jax.vjp(gelu_tanh, hidden)
    grad_hidden = pullback(cotangent[0].astype(jnp.float32))[0]
    grad_round = grad_hidden.astype(jnp.bfloat16)
    local_self = jnp.einsum("nd,nh->dh", own_feats, grad_round, preferred_element_type=jnp.float32)
    local_neigh = jnp.einsum("nd,nh->dh", neighbors, grad_round, preferred_element_type=jnp.float32)
    local_bias = jnp.sum(grad_round.astype(jnp.float32), axis=0)
    hid = local_bias.shape[0]
    weight_pack = jnp.concatenate(
        [local_self, local_neigh, jnp.broadcast_to(local_bias[None], (8, hid))], axis=0
    )
    steps = exchange_steps(("col", "row"))
    cross_step = [step for step in steps if step[0] == "col"][0]
    grad_agg = (
        jnp.einsum("nh,dh->nd", grad_round, w_neigh, preferred_element_type=jnp.float32)
        / divisor[:, None]
    )
    grad_agg = grad_agg.astype(jnp.bfloat16)
    adjoint_panel = lax.all_gather(grad_agg, "col", axis=0, tiled=True)
    weight_pack = exchange_add(weight_pack, steps[0])
    weight_pack, adjoint_panel = lax.optimization_barrier((weight_pack, adjoint_panel))
    panel = adjoint_panel.reshape(panel_blocks, block_size, feat_width)
    groups = adjacency.shape[0] // BACKWARD_GROUP
    half = groups // 2
    per_slot, panel_t = aggregate_backward(
        live_count, block_rows, block_slots, adjacency, panel, None, fetch_total, 0, half, False
    )
    weight_pack = exchange_add(weight_pack, steps[1])
    weight_pack, per_slot = lax.optimization_barrier((weight_pack, per_slot))
    per_slot = aggregate_backward(
        live_count, block_rows, block_slots, adjacency, panel_t, per_slot, fetch_total, half, groups, True
    )
    weight_pack = exchange_add(weight_pack, steps[2])
    weight_pack, per_slot = lax.optimization_barrier((weight_pack, per_slot))
    per_slot = per_slot.reshape(row_count, picks_each, block_size, feat_width)
    returned = spread(per_slot, "row")
    weight_pack = exchange_add(weight_pack, cross_step)
    weight_pack, returned = lax.optimization_barrier((weight_pack, returned))
    incoming = group_rows(
        asked_for[spread_sources("row")].reshape(-1),
        returned.reshape(fetch_total, block_size, feat_width),
        owned_count,
    )
    incoming = incoming.reshape(node_count, feat_width)
    grad_feats = (
        jnp.einsum("nh,dh->nd", grad_round, w_self, preferred_element_type=jnp.float32) + incoming
    )
    for step in steps[3:]:
        if step != cross_step:
            weight_pack = exchange_add(weight_pack, step)
    factor = 1.0 / math.sqrt(node_count * row_count * col_count)
    grad_self = weight_pack[:feat_width] * factor
    grad_neigh = weight_pack[feat_width : 2 * feat_width] * factor
    grad_bias = weight_pack[2 * feat_width] * factor
    return (
        output.astype(jnp.bfloat16)[None],
        grad_feats.astype(jnp.bfloat16)[None],
        grad_self,
        grad_neigh,
        grad_bias,
    )


def solution(mesh):
    return jax.shard_map(
        on_device,
        mesh=mesh,
        in_specs=(
            P("col", "row", None),
            P(),
            P(),
            P(),
            P("row", "col", None, None, None),
            P("row", "col", None),
            P("row", "col", None),
            P("row", "col", None),
            P("row", "col", None, None),
            P("col", "row", None),
        ),
        out_specs=(P("col", "row", None), P("col", "row", None), P(), P(), P()),
        check_vma=False,
    )
```

```python
import functools
import math

import jax
import jax.numpy as jnp
from jax import lax
from jax.experimental import pallas as pl
from jax.experimental.pallas import tpu as pltpu
from jax.sharding import PartitionSpec as P


FORWARD_GROUP = 160
BACKWARD_GROUP = 80
DEGREE_ROWS = 16


def gelu_tanh(values):
    return jax.nn.gelu(values, approximate=True)


def select_rows(indices, table, total):
    picker = (indices[:, None] == jnp.arange(total, dtype=jnp.int32)[None, :]).astype(table.dtype)
    flat = table.reshape(total, -1)
    taken = jnp.dot(picker, flat, preferred_element_type=jnp.float32).astype(table.dtype)
    return taken.reshape((indices.shape[0],) + table.shape[1:])


def group_rows(indices, values, total):
    grouper = (jnp.arange(total, dtype=jnp.int32)[:, None] == indices[None, :]).astype(jnp.float32)
    flat = values.reshape(values.shape[0], -1)
    added = jnp.dot(
        grouper, flat, precision=lax.Precision.HIGHEST, preferred_element_type=jnp.float32
    )
    return added.reshape((total,) + values.shape[1:])


def _live_group(g, count_ref, group):
    return jnp.minimum(g, (count_ref[0] - 1) // group)


def _forward_kernel(count_ref, row_ref, slot_ref, blk_ref, feat_ref, deg_ref, out_ref):
    g = pl.program_id(0)
    bs = blk_ref.shape[-1]
    node_count = out_ref.shape[1] - deg_ref.shape[1]
    owned = node_count // bs

    @pl.when(g == 0)
    def _():
        out_ref[:, :node_count, :] = jnp.zeros(
            (out_ref.shape[0], node_count, out_ref.shape[2]), jnp.float32
        )
        out_ref[:, node_count:, :] = deg_ref[...]

    count = count_ref[0]

    @pl.when(g * FORWARD_GROUP < count)
    def _():
        for j in range(FORWARD_GROUP):
            k = g * FORWARD_GROUP + j
            live = k < count
            r = row_ref[k]
            s = slot_ref[k]
            at = pl.multiple_of((r % owned) * bs, bs)
            prod = jnp.dot(blk_ref[j], feat_ref[s], preferred_element_type=jnp.float32)
            out_ref[r // owned, pl.ds(at, bs), :] += jnp.where(live, prod, 0.0)


def _backward_kernel(first, count_ref, row_ref, slot_ref, blk_ref, grad_ref, *refs):
    if len(refs) == 4:
        prev_ref, out_ref, gt_ref, acc_ref = refs
    else:
        prev_ref = None
        out_ref, gt_ref, acc_ref = refs
    g = pl.program_id(0) + first

    @pl.when(pl.program_id(0) == 0)
    def _():
        for r in range(grad_ref.shape[0]):
            gt_ref[r] = grad_ref[r].T
        acc_ref[...] = jnp.zeros_like(acc_ref)

    count = count_ref[0]

    @pl.when(g * BACKWARD_GROUP < count)
    def _():
        for j in range(BACKWARD_GROUP):
            k = g * BACKWARD_GROUP + j
            live = k < count
            r = row_ref[k]
            s = slot_ref[k]
            prod = jnp.dot(gt_ref[r], blk_ref[j], preferred_element_type=jnp.float32)
            acc_ref[s] += jnp.where(live, prod, 0.0)

    @pl.when(pl.program_id(0) == pl.num_programs(0) - 1)
    def _():
        for s in range(out_ref.shape[0]):
            if prev_ref is None:
                out_ref[s] = acc_ref[s].T
            else:
                out_ref[s] = acc_ref[s].T + prev_ref[s]


def aggregate_forward(counts, rows, slots, blocks, fetched, degree_rows, node_count):
    slot_total, bs, _ = blocks.shape
    fetch_total, _, width = fetched.shape
    chunks, pad, _ = degree_rows.shape
    out_rows = node_count + pad

    def block_at(g, c, r, s):
        return (_live_group(g, c, FORWARD_GROUP), 0, 0)

    grid_spec = pltpu.PrefetchScalarGridSpec(
        num_scalar_prefetch=3,
        grid=(slot_total // FORWARD_GROUP,),
        in_specs=[
            pl.BlockSpec((FORWARD_GROUP, bs, bs), block_at),
            pl.BlockSpec((fetch_total, bs, width), lambda g, c, r, s: (0, 0, 0)),
            pl.BlockSpec((chunks, pad, width), lambda g, c, r, s: (0, 0, 0)),
        ],
        out_specs=pl.BlockSpec((chunks, out_rows, width), lambda g, c, r, s: (0, 0, 0)),
    )
    return pl.pallas_call(
        _forward_kernel,
        grid_spec=grid_spec,
        out_shape=jax.ShapeDtypeStruct((chunks, out_rows, width), jnp.float32),
        compiler_params=pltpu.CompilerParams(dimension_semantics=("arbitrary",)),
        cost_estimate=pl.CostEstimate(
            flops=2 * slot_total * bs * bs * width,
            bytes_accessed=blocks.size * 2 + fetched.size * 2 + chunks * out_rows * width * 4,
            transcendentals=0,
        ),
    )(counts, rows, slots, blocks, fetched, degree_rows)


def aggregate_backward(counts, rows, slots, blocks, grad_panel, previous, fetch_total, first, last):
    slot_total, bs, _ = blocks.shape
    panel_blocks, _, width = grad_panel.shape
    extra = [] if previous is None else [previous]

    def block_at(g, c, r, s):
        return (_live_group(g + first, c, BACKWARD_GROUP), 0, 0)

    grid_spec = pltpu.PrefetchScalarGridSpec(
        num_scalar_prefetch=3,
        grid=(last - first,),
        in_specs=[
            pl.BlockSpec((BACKWARD_GROUP, bs, bs), block_at),
            pl.BlockSpec((panel_blocks, bs, width), lambda g, c, r, s: (0, 0, 0)),
        ]
        + [pl.BlockSpec((fetch_total, bs, width), lambda g, c, r, s: (0, 0, 0))] * len(extra),
        out_specs=pl.BlockSpec((fetch_total, bs, width), lambda g, c, r, s: (0, 0, 0)),
        scratch_shapes=[
            pltpu.VMEM((panel_blocks, width, bs), jnp.bfloat16),
            pltpu.VMEM((fetch_total, width, bs), jnp.float32),
        ],
    )
    share = (last - first) * BACKWARD_GROUP
    return pl.pallas_call(
        functools.partial(_backward_kernel, first),
        grid_spec=grid_spec,
        out_shape=jax.ShapeDtypeStruct((fetch_total, bs, width), jnp.float32),
        compiler_params=pltpu.CompilerParams(dimension_semantics=("arbitrary",)),
        cost_estimate=pl.CostEstimate(
            flops=2 * share * bs * bs * width,
            bytes_accessed=share * bs * bs * 2 + grad_panel.size * 2 + fetch_total * bs * width * 8,
            transcendentals=0,
        ),
    )(counts, rows, slots, blocks, grad_panel, *extra)


def exchange_steps(axes):
    steps = []
    for name in axes:
        size = lax.axis_size(name)
        step = 1
        while step < size:
            steps.append((name, size, step))
            step *= 2
    return steps[::-1]


def spread(chunks, name):
    size = lax.axis_size(name)
    me = lax.axis_index(name)
    received = [chunks[me]]
    for offset in range(1, size):
        pairs = [(i, (i + offset) % size) for i in range(size)]
        received.append(lax.ppermute(chunks[(me + offset) % size], name, pairs))
    return jnp.stack(received)


def scatter_sum(chunks, name):
    size = lax.axis_size(name)
    me = lax.axis_index(name)

    def swap(values, offset):
        return lax.ppermute(values, name, [(i, i ^ offset) for i in range(size)])

    def pick(values, index):
        return lax.dynamic_index_in_dim(values, index, axis=1, keepdims=False)

    offset = 1
    while chunks.shape[0] > 1:
        mine = (me // offset) % 2
        if chunks.shape[0] == 2:
            chunks = (pick(chunks[None], mine) + swap(pick(chunks[None], 1 - mine), offset))[0:1]
            break
        upper = (me // (2 * offset)) % 2
        quad = chunks.reshape((chunks.shape[0] // 4, 2, 2) + chunks.shape[1:])
        leaving = pick(quad, 1 - upper)
        leaving = pick(leaving, mine) + swap(pick(leaving, 1 - mine), offset)
        staying = pick(quad, upper)
        leaving, staying = lax.optimization_barrier((leaving, staying))
        staying = pick(staying, mine) + swap(pick(staying, 1 - mine), offset)
        chunks = staying + swap(leaving, 2 * offset)
        offset *= 4
    return chunks[0]


def spread_sources(name):
    size = lax.axis_size(name)
    me = lax.axis_index(name)
    return (me - jnp.arange(size, dtype=jnp.int32)) % size


def exchange_add(values, step):
    name, size, offset = step
    pairs = [(i, i ^ offset) for i in range(size)]
    return values + lax.ppermute(values, name, pairs)


def on_device(
    features, w_self, w_neigh, bias, blocks, blk_row, blk_slot, counts, col_list, cotangent
):
    own_feats = features[0]
    node_count, feat_width = own_feats.shape
    block_size = blocks.shape[-1]
    owned_count = node_count // block_size
    row_count = lax.axis_size("row")
    col_count = lax.axis_size("col")
    picks_each = col_list.shape[-1]
    fetch_total = row_count * picks_each
    panel_blocks = col_count * owned_count
    wanted = col_list[0, 0]
    asked_for = lax.all_to_all(wanted, "row", split_axis=0, concat_axis=0, tiled=True)
    block_rows = blk_row[0, 0]
    block_slots = blk_slot[0, 0]
    live_count = counts[0, 0]
    own_blocks = own_feats.reshape(owned_count, block_size, feat_width)
    outgoing = select_rows(asked_for.reshape(-1), own_blocks, owned_count)
    outgoing = outgoing.reshape(row_count, picks_each, block_size, feat_width)
    arrived = lax.all_to_all(outgoing, "row", split_axis=0, concat_axis=0, tiled=True)
    fetched = arrived.reshape(fetch_total, block_size, feat_width)
    adjacency = blocks[0, 0]
    live_rows = jnp.where(
        (jnp.arange(adjacency.shape[0]) < live_count[0])[:, None],
        jnp.sum(adjacency, axis=2, dtype=jnp.float32),
        0.0,
    )
    part_deg = group_rows(block_rows, live_rows, panel_blocks)
    part_deg = part_deg.reshape(col_count, owned_count, block_size)
    part_deg = jnp.pad(part_deg, ((0, 0), (0, DEGREE_ROWS - owned_count), (0, 0)))
    packed = aggregate_forward(
        live_count, block_rows, block_slots, adjacency, fetched, part_deg, node_count
    )
    reduced = scatter_sum(packed, "col")
    summed = reduced[:node_count]
    degree = reduced[node_count : node_count + owned_count].reshape(node_count)
    divisor = 1.0 + degree
    neighbors = (summed / divisor[:, None]).astype(jnp.bfloat16)
    hidden = (
        jnp.dot(own_feats, w_self, preferred_element_type=jnp.float32)
        + jnp.dot(neighbors, w_neigh, preferred_element_type=jnp.float32)
        + bias
    )
    output, pullback = jax.vjp(gelu_tanh, hidden)
    grad_hidden = pullback(cotangent[0].astype(jnp.float32))[0]
    grad_round = grad_hidden.astype(jnp.bfloat16)
    local_self = jnp.einsum("nd,nh->dh", own_feats, grad_round, preferred_element_type=jnp.float32)
    local_neigh = jnp.einsum("nd,nh->dh", neighbors, grad_round, preferred_element_type=jnp.float32)
    local_bias = jnp.sum(grad_round.astype(jnp.float32), axis=0)
    hid = local_bias.shape[0]
    weight_pack = jnp.concatenate(
        [local_self, local_neigh, jnp.broadcast_to(local_bias[None], (8, hid))], axis=0
    )
    steps = exchange_steps(("col", "row"))
    cross_step = [step for step in steps if step[0] == "col"][0]
    grad_agg = (
        jnp.einsum("nh,dh->nd", grad_round, w_neigh, preferred_element_type=jnp.float32)
        / divisor[:, None]
    )
    grad_agg = grad_agg.astype(jnp.bfloat16)
    adjoint_panel = lax.all_gather(grad_agg, "col", axis=0, tiled=True)
    weight_pack = exchange_add(weight_pack, steps[0])
    weight_pack, adjoint_panel = lax.optimization_barrier((weight_pack, adjoint_panel))
    panel = adjoint_panel.reshape(panel_blocks, block_size, feat_width)
    groups = adjacency.shape[0] // BACKWARD_GROUP
    half = groups // 2
    per_slot = aggregate_backward(
        live_count, block_rows, block_slots, adjacency, panel, None, fetch_total, 0, half
    )
    weight_pack = exchange_add(weight_pack, steps[1])
    weight_pack, per_slot = lax.optimization_barrier((weight_pack, per_slot))
    per_slot = aggregate_backward(
        live_count, block_rows, block_slots, adjacency, panel, per_slot, fetch_total, half, groups
    )
    weight_pack = exchange_add(weight_pack, steps[2])
    weight_pack, per_slot = lax.optimization_barrier((weight_pack, per_slot))
    per_slot = per_slot.reshape(row_count, picks_each, block_size, feat_width)
    returned = spread(per_slot, "row")
    weight_pack = exchange_add(weight_pack, cross_step)
    weight_pack, returned = lax.optimization_barrier((weight_pack, returned))
    incoming = group_rows(
        asked_for[spread_sources("row")].reshape(-1),
        returned.reshape(fetch_total, block_size, feat_width),
        owned_count,
    )
    incoming = incoming.reshape(node_count, feat_width)
    grad_feats = (
        jnp.einsum("nh,dh->nd", grad_round, w_self, preferred_element_type=jnp.float32) + incoming
    )
    for step in steps[3:]:
        if step != cross_step:
            weight_pack = exchange_add(weight_pack, step)
    factor = 1.0 / math.sqrt(node_count * row_count * col_count)
    grad_self = weight_pack[:feat_width] * factor
    grad_neigh = weight_pack[feat_width : 2 * feat_width] * factor
    grad_bias = weight_pack[2 * feat_width] * factor
    return (
        output.astype(jnp.bfloat16)[None],
        grad_feats.astype(jnp.bfloat16)[None],
        grad_self,
        grad_neigh,
        grad_bias,
    )


def solution(mesh):
    return jax.shard_map(
        on_device,
        mesh=mesh,
        in_specs=(
            P("col", "row", None),
            P(),
            P(),
            P(),
            P("row", "col", None, None, None),
            P("row", "col", None),
            P("row", "col", None),
            P("row", "col", None),
            P("row", "col", None, None),
            P("col", "row", None),
        ),
        out_specs=(P("col", "row", None), P("col", "row", None), P(), P(), P()),
        check_vma=False,
    )
```

```python
import functools
import math

import jax
import jax.numpy as jnp
from jax import lax
from jax.experimental import pallas as pl
from jax.experimental.pallas import tpu as pltpu
from jax.sharding import PartitionSpec as P


FORWARD_GROUP = 160
BACKWARD_GROUP = 80
DEGREE_ROWS = 16


def gelu_tanh(values):
    return jax.nn.gelu(values, approximate=True)


def select_rows(indices, table, total):
    picker = (indices[:, None] == jnp.arange(total, dtype=jnp.int32)[None, :]).astype(table.dtype)
    flat = table.reshape(total, -1)
    taken = jnp.dot(picker, flat, preferred_element_type=jnp.float32).astype(table.dtype)
    return taken.reshape((indices.shape[0],) + table.shape[1:])


def group_rows(indices, values, total):
    grouper = (jnp.arange(total, dtype=jnp.int32)[:, None] == indices[None, :]).astype(jnp.float32)
    flat = values.reshape(values.shape[0], -1)
    added = jnp.dot(
        grouper, flat, precision=lax.Precision.HIGHEST, preferred_element_type=jnp.float32
    )
    return added.reshape((total,) + values.shape[1:])


def _live_group(g, count_ref, group):
    return jnp.minimum(g, (count_ref[0] - 1) // group)


def _forward_kernel(count_ref, row_ref, slot_ref, blk_ref, feat_ref, deg_ref, out_ref):
    g = pl.program_id(0)
    bs = blk_ref.shape[-1]
    node_count = out_ref.shape[1] - deg_ref.shape[1]
    owned = node_count // bs

    @pl.when(g == 0)
    def _():
        out_ref[:, :node_count, :] = jnp.zeros(
            (out_ref.shape[0], node_count, out_ref.shape[2]), jnp.float32
        )
        out_ref[:, node_count:, :] = deg_ref[...]

    count = count_ref[0]

    @pl.when(g * FORWARD_GROUP < count)
    def _():
        for j in range(FORWARD_GROUP):
            k = g * FORWARD_GROUP + j
            live = k < count
            r = row_ref[k]
            s = slot_ref[k]
            at = pl.multiple_of((r % owned) * bs, bs)
            prod = jnp.dot(blk_ref[j], feat_ref[s], preferred_element_type=jnp.float32)
            out_ref[r // owned, pl.ds(at, bs), :] += jnp.where(live, prod, 0.0)


def _backward_kernel(first, count_ref, row_ref, slot_ref, blk_ref, grad_ref, *refs):
    if len(refs) == 4:
        prev_ref, out_ref, gt_ref, acc_ref = refs
    else:
        prev_ref = None
        out_ref, gt_ref, acc_ref = refs
    g = pl.program_id(0) + first

    @pl.when(pl.program_id(0) == 0)
    def _():
        for r in range(grad_ref.shape[0]):
            gt_ref[r] = grad_ref[r].T
        acc_ref[...] = jnp.zeros_like(acc_ref)

    count = count_ref[0]

    @pl.when(g * BACKWARD_GROUP < count)
    def _():
        for j in range(BACKWARD_GROUP):
            k = g * BACKWARD_GROUP + j
            live = k < count
            r = row_ref[k]
            s = slot_ref[k]
            prod = jnp.dot(gt_ref[r], blk_ref[j], preferred_element_type=jnp.float32)
            acc_ref[s] += jnp.where(live, prod, 0.0)

    @pl.when(pl.program_id(0) == pl.num_programs(0) - 1)
    def _():
        for s in range(out_ref.shape[0]):
            if prev_ref is None:
                out_ref[s] = acc_ref[s].T
            else:
                out_ref[s] = acc_ref[s].T + prev_ref[s]


def aggregate_forward(counts, rows, slots, blocks, fetched, degree_rows, node_count):
    slot_total, bs, _ = blocks.shape
    fetch_total, _, width = fetched.shape
    chunks, pad, _ = degree_rows.shape
    out_rows = node_count + pad

    def block_at(g, c, r, s):
        return (_live_group(g, c, FORWARD_GROUP), 0, 0)

    grid_spec = pltpu.PrefetchScalarGridSpec(
        num_scalar_prefetch=3,
        grid=(slot_total // FORWARD_GROUP,),
        in_specs=[
            pl.BlockSpec((FORWARD_GROUP, bs, bs), block_at),
            pl.BlockSpec((fetch_total, bs, width), lambda g, c, r, s: (0, 0, 0)),
            pl.BlockSpec((chunks, pad, width), lambda g, c, r, s: (0, 0, 0)),
        ],
        out_specs=pl.BlockSpec((chunks, out_rows, width), lambda g, c, r, s: (0, 0, 0)),
    )
    return pl.pallas_call(
        _forward_kernel,
        grid_spec=grid_spec,
        out_shape=jax.ShapeDtypeStruct((chunks, out_rows, width), jnp.float32),
        compiler_params=pltpu.CompilerParams(dimension_semantics=("arbitrary",)),
        cost_estimate=pl.CostEstimate(
            flops=2 * slot_total * bs * bs * width,
            bytes_accessed=blocks.size * 2 + fetched.size * 2 + chunks * out_rows * width * 4,
            transcendentals=0,
        ),
    )(counts, rows, slots, blocks, fetched, degree_rows)


def aggregate_backward(counts, rows, slots, blocks, grad_panel, previous, fetch_total, first, last):
    slot_total, bs, _ = blocks.shape
    panel_blocks, _, width = grad_panel.shape
    extra = [] if previous is None else [previous]

    def block_at(g, c, r, s):
        return (_live_group(g + first, c, BACKWARD_GROUP), 0, 0)

    grid_spec = pltpu.PrefetchScalarGridSpec(
        num_scalar_prefetch=3,
        grid=(last - first,),
        in_specs=[
            pl.BlockSpec((BACKWARD_GROUP, bs, bs), block_at),
            pl.BlockSpec((panel_blocks, bs, width), lambda g, c, r, s: (0, 0, 0)),
        ]
        + [pl.BlockSpec((fetch_total, bs, width), lambda g, c, r, s: (0, 0, 0))] * len(extra),
        out_specs=pl.BlockSpec((fetch_total, bs, width), lambda g, c, r, s: (0, 0, 0)),
        scratch_shapes=[
            pltpu.VMEM((panel_blocks, width, bs), jnp.bfloat16),
            pltpu.VMEM((fetch_total, width, bs), jnp.float32),
        ],
    )
    share = (last - first) * BACKWARD_GROUP
    return pl.pallas_call(
        functools.partial(_backward_kernel, first),
        grid_spec=grid_spec,
        out_shape=jax.ShapeDtypeStruct((fetch_total, bs, width), jnp.float32),
        compiler_params=pltpu.CompilerParams(dimension_semantics=("arbitrary",)),
        cost_estimate=pl.CostEstimate(
            flops=2 * share * bs * bs * width,
            bytes_accessed=share * bs * bs * 2 + grad_panel.size * 2 + fetch_total * bs * width * 8,
            transcendentals=0,
        ),
    )(counts, rows, slots, blocks, grad_panel, *extra)


def exchange_steps(axes):
    steps = []
    for name in axes:
        size = lax.axis_size(name)
        step = 1
        while step < size:
            steps.append((name, size, step))
            step *= 2
    return steps[::-1]


def spread(chunks, name):
    size = lax.axis_size(name)
    me = lax.axis_index(name)
    received = [chunks[me]]
    for offset in range(1, size):
        pairs = [(i, (i + offset) % size) for i in range(size)]
        received.append(lax.ppermute(chunks[(me + offset) % size], name, pairs))
    return jnp.stack(received)


def scatter_sum(chunks, name):
    size = lax.axis_size(name)
    me = lax.axis_index(name)

    def swap(values, offset):
        return lax.ppermute(values, name, [(i, i ^ offset) for i in range(size)])

    def pick(values, index):
        return lax.dynamic_index_in_dim(values, index, axis=1, keepdims=False)

    offset = 1
    while chunks.shape[0] > 1:
        mine = (me // offset) % 2
        if chunks.shape[0] == 2:
            chunks = (pick(chunks[None], mine) + swap(pick(chunks[None], 1 - mine), offset))[0:1]
            break
        upper = (me // (2 * offset)) % 2
        quad = chunks.reshape((chunks.shape[0] // 4, 2, 2) + chunks.shape[1:])
        leaving = pick(quad, 1 - upper)
        leaving = pick(leaving, mine) + swap(pick(leaving, 1 - mine), offset)
        staying = pick(quad, upper)
        leaving, staying = lax.optimization_barrier((leaving, staying))
        staying = pick(staying, mine) + swap(pick(staying, 1 - mine), offset)
        chunks = staying + swap(leaving, 2 * offset)
        offset *= 4
    return chunks[0]


def spread_sources(name):
    size = lax.axis_size(name)
    me = lax.axis_index(name)
    return (me - jnp.arange(size, dtype=jnp.int32)) % size


def exchange_add(values, step):
    name, size, offset = step
    pairs = [(i, i ^ offset) for i in range(size)]
    return values + lax.ppermute(values, name, pairs)


def on_device(
    features, w_self, w_neigh, bias, blocks, blk_row, blk_slot, counts, col_list, cotangent
):
    own_feats = features[0]
    node_count, feat_width = own_feats.shape
    block_size = blocks.shape[-1]
    owned_count = node_count // block_size
    row_count = lax.axis_size("row")
    col_count = lax.axis_size("col")
    picks_each = col_list.shape[-1]
    fetch_total = row_count * picks_each
    panel_blocks = col_count * owned_count
    wanted = col_list[0, 0]
    asked_for = lax.all_to_all(wanted, "row", split_axis=0, concat_axis=0, tiled=True)
    block_rows = blk_row[0, 0]
    block_slots = blk_slot[0, 0]
    live_count = counts[0, 0]
    own_blocks = own_feats.reshape(owned_count, block_size, feat_width)
    outgoing = select_rows(asked_for.reshape(-1), own_blocks, owned_count)
    outgoing = outgoing.reshape(row_count, picks_each, block_size, feat_width)
    arrived = lax.all_to_all(outgoing, "row", split_axis=0, concat_axis=0, tiled=True)
    fetched = arrived.reshape(fetch_total, block_size, feat_width)
    adjacency = blocks[0, 0]
    live_rows = jnp.where(
        (jnp.arange(adjacency.shape[0]) < live_count[0])[:, None],
        jnp.sum(adjacency, axis=2, dtype=jnp.float32),
        0.0,
    )
    part_deg = group_rows(block_rows, live_rows, panel_blocks)
    part_deg = part_deg.reshape(col_count, owned_count, block_size)
    part_deg = jnp.pad(part_deg, ((0, 0), (0, DEGREE_ROWS - owned_count), (0, 0)))
    packed = aggregate_forward(
        live_count, block_rows, block_slots, adjacency, fetched, part_deg, node_count
    )
    reduced = scatter_sum(packed, "col")
    summed = reduced[:node_count]
    degree = reduced[node_count : node_count + owned_count].reshape(node_count)
    divisor = 1.0 + degree
    neighbors = (summed / divisor[:, None]).astype(jnp.bfloat16)
    hidden = (
        jnp.dot(own_feats, w_self, preferred_element_type=jnp.float32)
        + jnp.dot(neighbors, w_neigh, preferred_element_type=jnp.float32)
        + bias
    )
    output, pullback = jax.vjp(gelu_tanh, hidden)
    grad_hidden = pullback(cotangent[0].astype(jnp.float32))[0]
    grad_round = grad_hidden.astype(jnp.bfloat16)
    local_self = jnp.einsum("nd,nh->dh", own_feats, grad_round, preferred_element_type=jnp.float32)
    local_neigh = jnp.einsum("nd,nh->dh", neighbors, grad_round, preferred_element_type=jnp.float32)
    local_bias = jnp.sum(grad_round.astype(jnp.float32), axis=0)
    hid = local_bias.shape[0]
    weight_pack = jnp.concatenate(
        [local_self, local_neigh, jnp.broadcast_to(local_bias[None], (8, hid))], axis=0
    )
    steps = exchange_steps(("col", "row"))
    cross_step = [step for step in steps if step[0] == "col"][0]
    grad_agg = (
        jnp.einsum("nh,dh->nd", grad_round, w_neigh, preferred_element_type=jnp.float32)
        / divisor[:, None]
    )
    grad_agg = grad_agg.astype(jnp.bfloat16)
    adjoint_panel = lax.all_gather(grad_agg, "col", axis=0, tiled=True)
    weight_pack = exchange_add(weight_pack, steps[0])
    weight_pack, adjoint_panel = lax.optimization_barrier((weight_pack, adjoint_panel))
    panel = adjoint_panel.reshape(panel_blocks, block_size, feat_width)
    groups = adjacency.shape[0] // BACKWARD_GROUP
    half = groups // 2
    per_slot = aggregate_backward(
        live_count, block_rows, block_slots, adjacency, panel, None, fetch_total, 0, half
    )
    weight_pack = exchange_add(weight_pack, steps[1])
    weight_pack, per_slot = lax.optimization_barrier((weight_pack, per_slot))
    per_slot = aggregate_backward(
        live_count, block_rows, block_slots, adjacency, panel, per_slot, fetch_total, half, groups
    )
    weight_pack = exchange_add(weight_pack, steps[2])
    self_term = jnp.einsum("nh,dh->nd", grad_round, w_self, preferred_element_type=jnp.float32)
    weight_pack, per_slot, self_term = lax.optimization_barrier((weight_pack, per_slot, self_term))
    per_slot = per_slot.reshape(row_count, picks_each, block_size, feat_width)
    returned = spread(per_slot, "row")
    weight_pack = exchange_add(weight_pack, cross_step)
    weight_pack, returned = lax.optimization_barrier((weight_pack, returned))
    incoming = group_rows(
        asked_for[spread_sources("row")].reshape(-1),
        returned.reshape(fetch_total, block_size, feat_width),
        owned_count,
    )
    incoming = incoming.reshape(node_count, feat_width)
    grad_feats = self_term + incoming
    for step in steps[3:]:
        if step != cross_step:
            weight_pack = exchange_add(weight_pack, step)
    factor = 1.0 / math.sqrt(node_count * row_count * col_count)
    grad_self = weight_pack[:feat_width] * factor
    grad_neigh = weight_pack[feat_width : 2 * feat_width] * factor
    grad_bias = weight_pack[2 * feat_width] * factor
    return (
        output.astype(jnp.bfloat16)[None],
        grad_feats.astype(jnp.bfloat16)[None],
        grad_self,
        grad_neigh,
        grad_bias,
    )


def solution(mesh):
    return jax.shard_map(
        on_device,
        mesh=mesh,
        in_specs=(
            P("col", "row", None),
            P(),
            P(),
            P(),
            P("row", "col", None, None, None),
            P("row", "col", None),
            P("row", "col", None),
            P("row", "col", None),
            P("row", "col", None, None),
            P("col", "row", None),
        ),
        out_specs=(P("col", "row", None), P("col", "row", None), P(), P(), P()),
        check_vma=False,
    )
```

```python
import functools
import math

import jax
import jax.numpy as jnp
from jax import lax
from jax.experimental import pallas as pl
from jax.experimental.pallas import tpu as pltpu
from jax.sharding import PartitionSpec as P


FORWARD_GROUP = 160
BACKWARD_GROUP = 80
DEGREE_ROWS = 16


def gelu_tanh(values):
    return jax.nn.gelu(values, approximate=True)


def select_rows(indices, table, total):
    picker = (indices[:, None] == jnp.arange(total, dtype=jnp.int32)[None, :]).astype(table.dtype)
    flat = table.reshape(total, -1)
    taken = jnp.dot(picker, flat, preferred_element_type=jnp.float32).astype(table.dtype)
    return taken.reshape((indices.shape[0],) + table.shape[1:])


def group_rows(indices, values, total):
    grouper = (jnp.arange(total, dtype=jnp.int32)[:, None] == indices[None, :]).astype(jnp.float32)
    flat = values.reshape(values.shape[0], -1)
    added = jnp.dot(
        grouper, flat, precision=lax.Precision.HIGHEST, preferred_element_type=jnp.float32
    )
    return added.reshape((total,) + values.shape[1:])


def _live_group(g, count_ref, group):
    return jnp.minimum(g, (count_ref[0] - 1) // group)


def _forward_kernel(count_ref, row_ref, slot_ref, blk_ref, feat_ref, deg_ref, out_ref):
    g = pl.program_id(0)
    bs = blk_ref.shape[-1]
    node_count = out_ref.shape[1] - deg_ref.shape[1]
    owned = node_count // bs

    @pl.when(g == 0)
    def _():
        out_ref[:, :node_count, :] = jnp.zeros(
            (out_ref.shape[0], node_count, out_ref.shape[2]), jnp.float32
        )
        out_ref[:, node_count:, :] = deg_ref[...]

    count = count_ref[0]

    @pl.when(g * FORWARD_GROUP < count)
    def _():
        for j in range(FORWARD_GROUP):
            k = g * FORWARD_GROUP + j
            live = k < count
            r = row_ref[k]
            s = slot_ref[k]
            at = pl.multiple_of((r % owned) * bs, bs)
            prod = jnp.dot(blk_ref[j], feat_ref[s], preferred_element_type=jnp.float32)
            out_ref[r // owned, pl.ds(at, bs), :] += jnp.where(live, prod, 0.0)


def _backward_kernel(first, count_ref, row_ref, slot_ref, blk_ref, grad_ref, *refs):
    if len(refs) == 4:
        prev_ref, out_ref, gt_ref, acc_ref = refs
    else:
        prev_ref = None
        out_ref, gt_ref, acc_ref = refs
    g = pl.program_id(0) + first

    @pl.when(pl.program_id(0) == 0)
    def _():
        for r in range(grad_ref.shape[0]):
            gt_ref[r] = grad_ref[r].T
        acc_ref[...] = jnp.zeros_like(acc_ref)

    count = count_ref[0]

    @pl.when(g * BACKWARD_GROUP < count)
    def _():
        for j in range(BACKWARD_GROUP):
            k = g * BACKWARD_GROUP + j
            live = k < count
            r = row_ref[k]
            s = slot_ref[k]
            prod = jnp.dot(gt_ref[r], blk_ref[j], preferred_element_type=jnp.float32)
            acc_ref[s] += jnp.where(live, prod, 0.0)

    @pl.when(pl.program_id(0) == pl.num_programs(0) - 1)
    def _():
        for s in range(out_ref.shape[0]):
            if prev_ref is None:
                out_ref[s] = acc_ref[s].T
            else:
                out_ref[s] = acc_ref[s].T + prev_ref[s]


def aggregate_forward(counts, rows, slots, blocks, fetched, degree_rows, node_count):
    slot_total, bs, _ = blocks.shape
    fetch_total, _, width = fetched.shape
    chunks, pad, _ = degree_rows.shape
    out_rows = node_count + pad

    def block_at(g, c, r, s):
        return (_live_group(g, c, FORWARD_GROUP), 0, 0)

    grid_spec = pltpu.PrefetchScalarGridSpec(
        num_scalar_prefetch=3,
        grid=(slot_total // FORWARD_GROUP,),
        in_specs=[
            pl.BlockSpec((FORWARD_GROUP, bs, bs), block_at),
            pl.BlockSpec((fetch_total, bs, width), lambda g, c, r, s: (0, 0, 0)),
            pl.BlockSpec((chunks, pad, width), lambda g, c, r, s: (0, 0, 0)),
        ],
        out_specs=pl.BlockSpec((chunks, out_rows, width), lambda g, c, r, s: (0, 0, 0)),
    )
    return pl.pallas_call(
        _forward_kernel,
        grid_spec=grid_spec,
        out_shape=jax.ShapeDtypeStruct((chunks, out_rows, width), jnp.float32),
        compiler_params=pltpu.CompilerParams(dimension_semantics=("arbitrary",)),
        cost_estimate=pl.CostEstimate(
            flops=2 * slot_total * bs * bs * width,
            bytes_accessed=blocks.size * 2 + fetched.size * 2 + chunks * out_rows * width * 4,
            transcendentals=0,
        ),
    )(counts, rows, slots, blocks, fetched, degree_rows)


def aggregate_backward(counts, rows, slots, blocks, grad_panel, previous, fetch_total, first, last):
    slot_total, bs, _ = blocks.shape
    panel_blocks, _, width = grad_panel.shape
    extra = [] if previous is None else [previous]

    def block_at(g, c, r, s):
        return (_live_group(g + first, c, BACKWARD_GROUP), 0, 0)

    grid_spec = pltpu.PrefetchScalarGridSpec(
        num_scalar_prefetch=3,
        grid=(last - first,),
        in_specs=[
            pl.BlockSpec((BACKWARD_GROUP, bs, bs), block_at),
            pl.BlockSpec((panel_blocks, bs, width), lambda g, c, r, s: (0, 0, 0)),
        ]
        + [pl.BlockSpec((fetch_total, bs, width), lambda g, c, r, s: (0, 0, 0))] * len(extra),
        out_specs=pl.BlockSpec((fetch_total, bs, width), lambda g, c, r, s: (0, 0, 0)),
        scratch_shapes=[
            pltpu.VMEM((panel_blocks, width, bs), jnp.bfloat16),
            pltpu.VMEM((fetch_total, width, bs), jnp.float32),
        ],
    )
    share = (last - first) * BACKWARD_GROUP
    return pl.pallas_call(
        functools.partial(_backward_kernel, first),
        grid_spec=grid_spec,
        out_shape=jax.ShapeDtypeStruct((fetch_total, bs, width), jnp.float32),
        compiler_params=pltpu.CompilerParams(dimension_semantics=("arbitrary",)),
        cost_estimate=pl.CostEstimate(
            flops=2 * share * bs * bs * width,
            bytes_accessed=share * bs * bs * 2 + grad_panel.size * 2 + fetch_total * bs * width * 8,
            transcendentals=0,
        ),
    )(counts, rows, slots, blocks, grad_panel, *extra)


def exchange_steps(axes):
    steps = []
    for name in axes:
        size = lax.axis_size(name)
        step = 1
        while step < size:
            steps.append((name, size, step))
            step *= 2
    return steps[::-1]


def spread(chunks, name):
    size = lax.axis_size(name)
    me = lax.axis_index(name)
    received = [chunks[me]]
    for offset in range(1, size):
        pairs = [(i, (i + offset) % size) for i in range(size)]
        received.append(lax.ppermute(chunks[(me + offset) % size], name, pairs))
    return jnp.stack(received)


def scatter_sum(chunks, name):
    size = lax.axis_size(name)
    me = lax.axis_index(name)

    def swap(values, offset):
        return lax.ppermute(values, name, [(i, i ^ offset) for i in range(size)])

    def pick(values, index):
        return lax.dynamic_index_in_dim(values, index, axis=1, keepdims=False)

    offset = 1
    while chunks.shape[0] > 1:
        mine = (me // offset) % 2
        if chunks.shape[0] == 2:
            chunks = (pick(chunks[None], mine) + swap(pick(chunks[None], 1 - mine), offset))[0:1]
            break
        upper = (me // (2 * offset)) % 2
        quad = chunks.reshape((chunks.shape[0] // 4, 2, 2) + chunks.shape[1:])
        leaving = pick(quad, 1 - upper)
        leaving = pick(leaving, mine) + swap(pick(leaving, 1 - mine), offset)
        staying = pick(quad, upper)
        leaving, staying = lax.optimization_barrier((leaving, staying))
        staying = pick(staying, mine) + swap(pick(staying, 1 - mine), offset)
        chunks = staying + swap(leaving, 2 * offset)
        offset *= 4
    return chunks[0]


def spread_sources(name):
    size = lax.axis_size(name)
    me = lax.axis_index(name)
    return (me - jnp.arange(size, dtype=jnp.int32)) % size


def exchange_add(values, step):
    name, size, offset = step
    pairs = [(i, i ^ offset) for i in range(size)]
    return values + lax.ppermute(values, name, pairs)


def on_device(
    features, w_self, w_neigh, bias, blocks, blk_row, blk_slot, counts, col_list, cotangent
):
    own_feats = features[0]
    node_count, feat_width = own_feats.shape
    block_size = blocks.shape[-1]
    owned_count = node_count // block_size
    row_count = lax.axis_size("row")
    col_count = lax.axis_size("col")
    picks_each = col_list.shape[-1]
    fetch_total = row_count * picks_each
    panel_blocks = col_count * owned_count
    wanted = col_list[0, 0]
    asked_for = lax.all_to_all(wanted, "row", split_axis=0, concat_axis=0, tiled=True)
    block_rows = blk_row[0, 0]
    block_slots = blk_slot[0, 0]
    live_count = counts[0, 0]
    own_blocks = own_feats.reshape(owned_count, block_size, feat_width)
    outgoing = select_rows(asked_for.reshape(-1), own_blocks, owned_count)
    outgoing = outgoing.reshape(row_count, picks_each, block_size, feat_width)
    arrived = lax.all_to_all(outgoing, "row", split_axis=0, concat_axis=0, tiled=True)
    fetched = arrived.reshape(fetch_total, block_size, feat_width)
    adjacency = blocks[0, 0]
    live_rows = jnp.where(
        (jnp.arange(adjacency.shape[0]) < live_count[0])[:, None],
        jnp.sum(adjacency, axis=2, dtype=jnp.float32),
        0.0,
    )
    part_deg = group_rows(block_rows, live_rows, panel_blocks)
    part_deg = part_deg.reshape(col_count, owned_count, block_size)
    part_deg = jnp.pad(part_deg, ((0, 0), (0, DEGREE_ROWS - owned_count), (0, 0)))
    packed = aggregate_forward(
        live_count, block_rows, block_slots, adjacency, fetched, part_deg, node_count
    )
    reduced = scatter_sum(packed, "col")
    summed = reduced[:node_count]
    degree = reduced[node_count : node_count + owned_count].reshape(node_count)
    divisor = 1.0 + degree
    neighbors = (summed / divisor[:, None]).astype(jnp.bfloat16)
    hidden = (
        jnp.dot(own_feats, w_self, preferred_element_type=jnp.float32)
        + jnp.dot(neighbors, w_neigh, preferred_element_type=jnp.float32)
        + bias
    )
    output, pullback = jax.vjp(gelu_tanh, hidden)
    grad_hidden = pullback(cotangent[0].astype(jnp.float32))[0]
    grad_round = grad_hidden.astype(jnp.bfloat16)
    local_self = jnp.einsum("nd,nh->dh", own_feats, grad_round, preferred_element_type=jnp.float32)
    local_neigh = jnp.einsum("nd,nh->dh", neighbors, grad_round, preferred_element_type=jnp.float32)
    local_bias = jnp.sum(grad_round.astype(jnp.float32), axis=0)
    hid = local_bias.shape[0]
    weight_pack = jnp.concatenate(
        [local_self, local_neigh, jnp.broadcast_to(local_bias[None], (8, hid))], axis=0
    )
    steps = exchange_steps(("col", "row"))
    cross_step = [step for step in steps if step[0] == "col"][0]
    grad_agg = (
        jnp.einsum("nh,dh->nd", grad_round, w_neigh, preferred_element_type=jnp.float32)
        / divisor[:, None]
    )
    grad_agg = grad_agg.astype(jnp.bfloat16)
    adjoint_panel = lax.all_gather(grad_agg, "col", axis=0, tiled=True)
    weight_pack = exchange_add(weight_pack, steps[0])
    weight_pack, adjoint_panel = lax.optimization_barrier((weight_pack, adjoint_panel))
    panel = adjoint_panel.reshape(panel_blocks, block_size, feat_width)
    groups = adjacency.shape[0] // BACKWARD_GROUP
    half = groups // 2
    per_slot = aggregate_backward(
        live_count, block_rows, block_slots, adjacency, panel, None, fetch_total, 0, half
    )
    weight_pack = exchange_add(weight_pack, steps[1])
    weight_pack, per_slot = lax.optimization_barrier((weight_pack, per_slot))
    per_slot = aggregate_backward(
        live_count, block_rows, block_slots, adjacency, panel, per_slot, fetch_total, half, groups
    )
    weight_pack = exchange_add(weight_pack, steps[2])
    weight_pack, per_slot = lax.optimization_barrier((weight_pack, per_slot))
    per_slot = per_slot.reshape(row_count, picks_each, block_size, feat_width)
    returned = spread(per_slot, "row")
    weight_pack = exchange_add(weight_pack, cross_step)
    for step in steps[3:]:
        if step != cross_step:
            weight_pack = exchange_add(weight_pack, step)
    factor = 1.0 / math.sqrt(node_count * row_count * col_count)
    grad_self = weight_pack[:feat_width] * factor
    grad_neigh = weight_pack[feat_width : 2 * feat_width] * factor
    grad_bias = weight_pack[2 * feat_width] * factor
    grad_self, grad_neigh, grad_bias, returned = lax.optimization_barrier(
        (grad_self, grad_neigh, grad_bias, returned)
    )
    incoming = group_rows(
        asked_for[spread_sources("row")].reshape(-1),
        returned.reshape(fetch_total, block_size, feat_width),
        owned_count,
    )
    incoming = incoming.reshape(node_count, feat_width)
    grad_feats = (
        jnp.einsum("nh,dh->nd", grad_round, w_self, preferred_element_type=jnp.float32) + incoming
    )
    return (
        output.astype(jnp.bfloat16)[None],
        grad_feats.astype(jnp.bfloat16)[None],
        grad_self,
        grad_neigh,
        grad_bias,
    )


def solution(mesh):
    return jax.shard_map(
        on_device,
        mesh=mesh,
        in_specs=(
            P("col", "row", None),
            P(),
            P(),
            P(),
            P("row", "col", None, None, None),
            P("row", "col", None),
            P("row", "col", None),
            P("row", "col", None),
            P("row", "col", None, None),
            P("col", "row", None),
        ),
        out_specs=(P("col", "row", None), P("col", "row", None), P(), P(), P()),
        check_vma=False,
    )
```
